512 devices in a mesh: dp: 128 (over x, z, core), bin: 4 (over y).
Axes of the slice: x: 4, y: 4, z: 16, core: 2. Of those that a mesh axis runs over, the one named last changes fastest.
Arguments:
- features: bfloat16 [65536, 2, 2048], P(('dp', 'bin')), may hold values from -90 to 90
- head_weight: bfloat16 [2048, 1024], P('bin'), may hold values from -9 to 9
- bin_of_row: int32 [65536, 1], P(('dp', 'bin')), may hold values from 0 to 191; in each aligned block of 128 rows (0 to 127, 128 to 255, ...) at most 2 rows name the same one
- bin_owner: int32 [192], replicated, may hold values from 0 to 127, never falling along the last dimension, each value on 1 to 2 neighbouring positions
- bin_link: int32 [192], replicated, may hold values 0 or 1
Outputs:
- grad_rows: bfloat16 [65536, 2, 1024], P(('dp', 'bin'))
- grad_weight: float32 [2048, 1024], P(('bin', 'dp'))
The draws below stay inside these ranges and needn't reach their ends.
Inputs may be any that keep to these rules, and one draw needn't show every extreme that they name: `bin_of_row`: in the rows of one device no bin appears more than 2 times. `bin_owner`: never falls; every owner holds 1 to 2 consecutive bins.
All inputs are finite; a program needn't handle non-finite values.
Results may differ from the reference program's by a relative error of at most 0.012.
Values may be sent and summed in bfloat16 or wider, within the bound.
No kernel may reach another device: no remote copies, remote signals or barrier semaphores. Data moves between devices by JAX's collectives and lax.ppermute only.
A program may use at most 64 MiB of HBM per device.

```python
import math
import jax
import jax.numpy as jnp
import numpy as np
from jax import lax

F = 2048
D = 1024
ROWS_DEV = 128
MOSTB = 2
NBINS = 192
CAP = 2
ROWS = 65536
N_DP = 128
N_BIN = 4


def draw_features(key, part):
    parts_of_key = jax.random.split(key, 3)
    base = jnp.clip(jax.random.normal(parts_of_key[0], (ROWS, F)), -5.0, 5.0)
    noise = jnp.clip(jax.random.normal(parts_of_key[1], (ROWS, F)), -5.0, 5.0)
    spread = jnp.exp(jax.random.uniform(parts_of_key[2], (ROWS, 1, 1), minval=0.0, maxval=2.302585))
    other = 0.8 * base + 0.6 * noise
    return (jnp.stack([base, other], axis=1) * spread).astype(jnp.bfloat16)


def draw_head_weight(key, part):
    parts_of_key = jax.random.split(key, 2)
    spread = jnp.exp(jax.random.uniform(parts_of_key[1], (1, D), minval=0.0, maxval=2.302585))
    entries = jnp.clip(jax.random.normal(parts_of_key[0], (F, D)), -5.0, 5.0)
    return (entries * spread / F ** 0.5).astype(jnp.bfloat16)


def with_ends(result, stream_key, smallest, top_value):
    longest = result.shape.index(max(result.shape))
    spots = []
    for shift in (0, 1):
        where = [jax.random.randint(jax.random.fold_in(stream_key, axis), (), 0, length) for axis, length in enumerate(result.shape)]
        where[longest] = (where[longest] + shift) % result.shape[longest]
        spots.append(tuple(where))
    return result.at[spots[0]].set(smallest).at[spots[1]].set(top_value)


def profile(count, total, bound, lean):
    portions = [(1 << 20) // math.isqrt(rank ** lean) + 1 for rank in range(2, count + 1)]
    spare, counts = total - bound - (count - 1), [1] * (count - 1)
    while spare > 0:
        candidates = [i for i in range(count - 1) if counts[i] < bound]
        whole, remaining = sum([portions[i] for i in candidates]), spare
        for i in candidates:
            more = min(bound - counts[i], max(1, remaining * portions[i] // whole), spare)
            counts[i] = counts[i] + more
            spare = spare - more
    return np.array([bound] + counts)


def uneven(stream_key, amount, total, most, lean):
    if amount == 2:
        one = jax.random.randint(stream_key, (), max(1, total - most), min(most, total - 1) + 1)
        return jnp.stack([one, total - one])
    sizes = jnp.asarray(profile(amount, total, most, lean), jnp.int32)
    pairs = (amount - 1) // 2
    source_of, taker = sizes[1:1 + 2 * pairs:2], sizes[2:2 + 2 * pairs:2]
    room = jnp.minimum(source_of - 1, most - taker)
    moved = jax.random.randint(jax.random.fold_in(stream_key, 1), (pairs,), 0, 1 << 20) % (room + 1)
    sizes = sizes.at[1:1 + 2 * pairs:2].set(source_of - moved).at[2:2 + 2 * pairs:2].set(taker + moved)
    return sizes[jax.random.permutation(jax.random.fold_in(stream_key, 2), amount)]


def deal_out(stream_key, own, number, rows, amount, top, limit, lean):
    ranking = jax.random.permutation(stream_key, amount)
    heavy_load, usual = load_shares(amount, rows * top, limit, lean, True), load_shares(amount, rows * top, limit, lean, False)
    places = jnp.arange(amount)

    def named(lengths, rotation):
        used = int((lengths > 0).sum())
        fixed = max(1, used // 4)
        shifted = fixed + (places - fixed + rotation * (used - fixed)) % max(1, amount - fixed)
        return jnp.zeros((amount,), jnp.int32).at[ranking[jnp.where(places < fixed, places, shifted)]].set(jnp.asarray(lengths, jnp.int32))

    lengths = jnp.where(number % 4 == 0, named(heavy_load, number // 4), named(usual, number - number // 4 - 1))
    mixed = jax.random.permutation(jax.random.fold_in(own, 3), amount)
    donor, sink = mixed[0:amount // 2 * 2:2], mixed[1:amount // 2 * 2:2]
    slack = jnp.minimum(lengths[donor] - 1, limit - lengths[sink]) // 2
    slack = jnp.where((donor == ranking[0]) | (sink == ranking[0]) | (lengths[sink] == 0), 0, jnp.maximum(slack, 0))
    shifted = jax.random.randint(jax.random.fold_in(own, 4), (amount // 2,), 0, 1 << 20) % (slack + 1)
    lengths = lengths.at[donor].add(-shifted).at[sink].add(shifted)
    items = jnp.searchsorted(jnp.cumsum(lengths), jnp.arange(rows * top), side="right").astype(jnp.int32)
    table = items.reshape(top, rows).T
    table = table[jax.random.permutation(jax.random.fold_in(own, 1), rows)]
    rotation = jax.random.randint(jax.random.fold_in(own, 2), (rows, 1), 0, top)
    return jnp.take_along_axis(table, (jnp.arange(top)[None, :] + rotation) % top, axis=1)


def load_shares(number_of, total, reach, slope, full):
    portions = [(1 << 20) // math.isqrt(standing ** slope) + 1 for standing in range(1, number_of + 1)]
    largest = reach if full else min(reach, max(-(-total // number_of), total * portions[0] // sum(portions)))
    least = 1 if total - largest >= number_of - 1 else 0
    given, surplus = [largest] + [least] * (number_of - 1), total - largest - least * (number_of - 1)
    while surplus > 0:
        movable = [i for i in range(1, number_of) if given[i] < largest] or [i for i in range(1, number_of) if given[i] < reach]
        pool, budget = sum([portions[i] for i in movable]), surplus
        for i in movable:
            more = min(reach - given[i], max(1, budget * portions[i] // pool), surplus)
            given[i] = given[i] + more
            surplus = surplus - more
    return np.array(given)


def setup_inputs(seed: int = 0) -> dict:
    keys = jax.random.split(jax.random.key(seed), 6)
    features = draw_features(jax.random.fold_in(keys[5], 71), 0)
    head_weight = draw_head_weight(jax.random.fold_in(keys[5], 71), 0)
    bin_of_row_keys = jax.random.split(jax.random.fold_in(keys[2], 1), ROWS // ROWS_DEV)
    bin_of_row_turns = jax.random.permutation(jax.random.fold_in(keys[2], 3), ROWS // ROWS_DEV)
    bin_of_row = jax.vmap(lambda own, number: deal_out(jax.random.fold_in(keys[2], 2), own, number, ROWS_DEV, NBINS, 1, CAP, 2))(bin_of_row_keys, bin_of_row_turns).reshape((ROWS, 1))
    bin_owner = jnp.searchsorted(jnp.cumsum(uneven(keys[3], N_DP, NBINS, MOSTB, 1)), jnp.arange(NBINS), side="right").astype(jnp.int32)
    bin_link = with_ends((jax.random.randint(keys[4], (NBINS,), 0, 2) < 1).astype(jnp.int32), jax.random.fold_in(keys[4], 1), 0, 1)
    return {"features": features, "head_weight": head_weight, "bin_of_row": bin_of_row, "bin_owner": bin_owner, "bin_link": bin_link}


SOFTMAX_TEMP_SCALE = 0.1

def allowed_mask(valid, first, bin_link, group_slots, per_bin):
    per_owner = per_bin * MOSTB
    position = jnp.arange(group_slots, dtype=jnp.int32)
    local_bin = position % per_owner // per_bin
    padded = jnp.concatenate([bin_link.astype(jnp.int32), jnp.zeros((MOSTB,), jnp.int32)])
    nearby = lax.dynamic_slice(padded, (first,), (MOSTB,))
    lower = jnp.minimum(local_bin[:, None], local_bin[None, :])
    linked = jnp.zeros((group_slots, group_slots), jnp.int32)
    for height in range(MOSTB):
        linked = linked + jnp.where(lower == height, nearby[height], 0)
    spacing = jnp.abs(local_bin[:, None] - local_bin[None, :])
    paired = valid[:, None] & valid[None, :]
    allowed = paired & ((spacing == 0) | (spacing == 1) & (linked == 1))
    allowed = allowed | (position[:, None] == position[None, :])
    return allowed.astype(jnp.float32)

def contrast(query_rows, key_matrix, allowed, valid):
    similarity_scores = lax.dot_general(query_rows, key_matrix, (((1,), (1,)), ((), ())), preferred_element_type=jnp.float32) / SOFTMAX_TEMP_SCALE
    weights = allowed * jnp.exp(similarity_scores)
    shares = weights / lax.optimization_barrier(jnp.sum(weights, axis=1, keepdims=True))
    position = jnp.arange(query_rows.shape[0], dtype=jnp.int32)
    diagonal = (position[:, None] == position[None, :]).astype(jnp.float32)
    logit_gradient = ((shares - diagonal) * valid[:, None]).astype(jnp.bfloat16)
    query_gradient = (jnp.dot(logit_gradient, key_matrix, preferred_element_type=jnp.float32) / SOFTMAX_TEMP_SCALE).astype(jnp.bfloat16)
    key_gradient_rows = (lax.dot_general(logit_gradient, query_rows, (((0,), (0,)), ((), ())), preferred_element_type=jnp.float32) / SOFTMAX_TEMP_SCALE).astype(jnp.bfloat16)
    return jnp.stack([query_gradient, key_gradient_rows], axis=1)

def reference(features, head_weight, bin_of_row, bin_owner, bin_link):
    per_owner = CAP * MOSTB
    group_slots = N_DP * per_owner
    embedded = jnp.dot(features.reshape(ROWS * 2, F), head_weight, preferred_element_type=jnp.float32).reshape(ROWS, 2, D)
    scale = lax.rsqrt(lax.optimization_barrier(jnp.sum(embedded * embedded, axis=2, keepdims=True)) + 1e-06)
    unit = embedded * scale
    sent = unit.astype(jnp.bfloat16)
    row_bins = bin_of_row[:, 0].astype(jnp.int32)
    owner = bin_owner[row_bins].astype(jnp.int32)
    first_by_bin = lax.optimization_barrier(jnp.sum((bin_owner[None, :] < bin_owner[:, None]).astype(jnp.int32), axis=1)).astype(jnp.int32)
    local_bin = row_bins - first_by_bin[row_bins]
    per_device = row_bins.reshape(N_DP * N_BIN, ROWS_DEV)
    order = jnp.arange(ROWS_DEV, dtype=jnp.int32)
    earlier = (per_device[:, :, None] == per_device[:, None, :]) & (order[None, None, :] < order[None, :, None])
    seat = lax.optimization_barrier(jnp.sum(earlier.astype(jnp.int32), axis=2)).reshape(ROWS).astype(jnp.int32)
    device = jnp.arange(ROWS, dtype=jnp.int32) // ROWS_DEV
    group = owner * N_BIN + device % N_BIN
    position = (group * group_slots + device // N_BIN * per_owner + local_bin * CAP + seat).astype(jnp.int32)
    row_of = jnp.full((N_DP * N_BIN * group_slots,), ROWS, jnp.int32).at[position].set(jnp.arange(ROWS, dtype=jnp.int32))
    padded = jnp.concatenate([sent, jnp.zeros((1, 2, D), jnp.bfloat16)], axis=0)

    def visit(carry, index):
        members = lax.dynamic_slice(row_of, (index * group_slots,), (group_slots,))
        valid = members < ROWS
        first = jnp.sum((bin_owner < index // N_BIN).astype(jnp.int32)).astype(jnp.int32)
        allowed = allowed_mask(valid, first, bin_link, group_slots, CAP)
        picked = padded[members]
        grads = contrast(picked[:, 0], picked[:, 1], allowed, valid.astype(jnp.float32))
        return (carry.at[members].set(grads), None)
    start = jnp.zeros((ROWS + 1, 2, D), jnp.bfloat16)
    grads_pad, _ = lax.scan(visit, start, jnp.arange(N_DP * N_BIN, dtype=jnp.int32))
    row_grads = grads_pad[:ROWS].astype(jnp.float32)
    grad_rows = (scale * (row_grads - unit * lax.optimization_barrier(jnp.sum(unit * row_grads, axis=2, keepdims=True)))).astype(jnp.bfloat16)
    grad_weight = lax.dot_general(features.reshape(ROWS * 2, F), grad_rows.reshape(ROWS * 2, D), (((0,), (0,)), ((), ())), preferred_element_type=jnp.float32) / ROWS_DEV
    return (grad_rows, grad_weight)
```

```python
import jax
import jax.numpy as jnp
from jax import lax
from jax.sharding import Mesh
from jax.sharding import PartitionSpec as P

MOSTB = 2


SOFTMAX_TEMP_SCALE = 0.1

DP_PARTS = (("dx", 4), ("dz", 16), ("dc", 2))
DP = tuple(name for name, _ in DP_PARTS)
EMPTY_MARK = 4.0


def allowed_mask(valid, first, bin_link, group_slots, per_bin):
    per_owner = per_bin * MOSTB
    position = jnp.arange(group_slots, dtype=jnp.int32)
    local_bin = position % per_owner // per_bin
    padded = jnp.concatenate([bin_link, jnp.zeros((MOSTB,), jnp.int32)])
    nearby = lax.dynamic_slice(padded, (first,), (MOSTB,))
    lower = jnp.minimum(local_bin[:, None], local_bin[None, :])
    linked = jnp.zeros((group_slots, group_slots), jnp.int32)
    for height in range(MOSTB):
        linked = linked + jnp.where(lower == height, nearby[height], 0)
    spacing = jnp.abs(local_bin[:, None] - local_bin[None, :])
    paired = valid[:, None] & valid[None, :]
    allowed = paired & ((spacing == 0) | (spacing == 1) & (linked == 1))
    allowed = allowed | (position[:, None] == position[None, :])
    return allowed.astype(jnp.float32)


def contrast(query_rows, key_matrix, allowed, valid):
    similarity_scores = (
        lax.dot_general(
            query_rows, key_matrix, (((1,), (1,)), ((), ())), preferred_element_type=jnp.float32
        )
        / SOFTMAX_TEMP_SCALE
    )
    weights = allowed * jnp.exp(similarity_scores)
    shares = weights / jnp.sum(weights, axis=1, keepdims=True)
    position = jnp.arange(query_rows.shape[0], dtype=jnp.int32)
    diagonal = (position[:, None] == position[None, :]).astype(jnp.float32)
    logit_gradient = ((shares - diagonal) * valid[:, None]).astype(jnp.bfloat16)
    query_gradient = (
        jnp.dot(logit_gradient, key_matrix, preferred_element_type=jnp.float32) / SOFTMAX_TEMP_SCALE
    ).astype(jnp.bfloat16)
    key_gradient_rows = (
        lax.dot_general(
            logit_gradient, query_rows, (((0,), (0,)), ((), ())), preferred_element_type=jnp.float32
        )
        / SOFTMAX_TEMP_SCALE
    ).astype(jnp.bfloat16)
    return jnp.stack([query_gradient, key_gradient_rows], axis=1)


def dp_index():
    index = 0
    for name, size in DP_PARTS:
        index = index * size + lax.axis_index(name)
    return index


def local(features, head_weight, bin_of_row, bin_owner, bin_link):
    rows_dev, views, feat_dim = features.shape
    part_rows, emb_dim = head_weight.shape
    sources = 1
    for _, size in DP_PARTS:
        sources *= size
    bins_n = lax.axis_size("bin")
    bin_count = bin_owner.shape[0]
    per_bin = max(2, 2 * rows_dev // bin_count)
    per_owner = per_bin * MOSTB
    group_slots = sources * per_owner
    flat = features.reshape(rows_dev * views, feat_dim)
    folded = jnp.dot(
        flat,
        lax.all_gather(head_weight, "bin", axis=0, tiled=True),
        preferred_element_type=jnp.float32,
    )
    embedded = folded.reshape(rows_dev, views, emb_dim)
    scale = lax.rsqrt(jnp.sum(embedded * embedded, axis=2, keepdims=True) + 1e-06)
    unit = embedded * scale
    sent = unit.astype(jnp.bfloat16)
    row_bins = bin_of_row[:, 0]
    lookup = row_bins[:, None] == jnp.arange(bin_count, dtype=jnp.int32)[None, :]
    owner = jnp.sum(jnp.where(lookup, bin_owner[None, :], 0), axis=1)
    first_by_bin = jnp.sum((bin_owner[None, :] < bin_owner[:, None]).astype(jnp.int32), axis=1)
    local_bin = row_bins - jnp.sum(jnp.where(lookup, first_by_bin[None, :], 0), axis=1)
    order = jnp.arange(rows_dev, dtype=jnp.int32)
    earlier = (row_bins[:, None] == row_bins[None, :]) & (order[None, :] < order[:, None])
    seat = jnp.sum(earlier.astype(jnp.int32), axis=1)
    target = owner * per_owner + local_bin * per_bin + seat
    empty = jnp.zeros((group_slots, views, emb_dim), jnp.bfloat16).at[:, 0, 0].set(EMPTY_MARK)
    outbox = empty.at[target].set(sent)
    inbox = lax.all_to_all(
        outbox.reshape(sources, per_owner, views, emb_dim),
        DP,
        split_axis=0,
        concat_axis=0,
        tiled=True,
    )
    inbox = inbox.reshape(group_slots, views, emb_dim)
    valid = inbox[:, 0, 0] < 2.0
    inbox = jnp.where(valid[:, None, None], inbox, jnp.zeros_like(inbox))
    first = jnp.sum((bin_owner < dp_index()).astype(jnp.int32))
    allowed = allowed_mask(valid, first, bin_link, group_slots, per_bin)
    grads = contrast(inbox[:, 0], inbox[:, 1], allowed, valid.astype(jnp.float32))
    returned = lax.all_to_all(
        grads.reshape(sources, per_owner, views, emb_dim),
        DP,
        split_axis=0,
        concat_axis=0,
        tiled=True,
    )
    row_grads = returned.reshape(group_slots, views, emb_dim)[target].astype(jnp.float32)
    grad_rows = (
        scale * (row_grads - unit * jnp.sum(unit * row_grads, axis=2, keepdims=True))
    ).astype(jnp.bfloat16)
    columns = lax.all_to_all(
        features.reshape(rows_dev, views, bins_n, part_rows),
        "bin",
        split_axis=2,
        concat_axis=0,
        tiled=True,
    )
    outgrad = lax.all_gather(grad_rows, "bin", axis=0, tiled=True)
    count = columns.shape[0]
    sizes = [size for _, size in DP_PARTS]
    columns = columns.reshape(count * views, *sizes, part_rows // sources)
    columns = jnp.transpose(columns, (0, 3, 2, 1, 4)).reshape(count * views, part_rows)
    local_grad = lax.dot_general(
        columns,
        outgrad.reshape(count * views, emb_dim),
        (((0,), (0,)), ((), ())),
        preferred_element_type=jnp.float32,
    )
    for name in ("dc", "dz", "dx"):
        local_grad = lax.psum_scatter(local_grad, name, scatter_dimension=0, tiled=True)
    grad_weight = local_grad / rows_dev
    return (grad_rows, grad_weight)


def solution(mesh):
    sizes = [size for _, size in DP_PARTS]
    devices = mesh.devices.reshape(*sizes, mesh.devices.shape[1])
    parted = Mesh(devices, (*DP, "bin"))
    return jax.shard_map(
        local,
        mesh=parted,
        in_specs=(P((*DP, "bin"), None, None), P("bin", None), P((*DP, "bin"), None), P(), P()),
        out_specs=(P((*DP, "bin"), None, None), P(("bin", *DP), None)),
        check_vma=False,
    )
```

```python
import jax
import jax.numpy as jnp
from jax import lax
from jax.sharding import Mesh
from jax.sharding import PartitionSpec as P

MOSTB = 2


SOFTMAX_TEMP_SCALE = 0.1

DP_PARTS = (("dx", 4), ("dz", 16), ("dc", 2))
DP = tuple(name for name, _ in DP_PARTS)
EMPTY_MARK = 4.0


def allowed_mask(valid, first, bin_link, group_slots, per_bin):
    per_owner = per_bin * MOSTB
    position = jnp.arange(group_slots, dtype=jnp.int32)
    local_bin = position % per_owner // per_bin
    padded = jnp.concatenate([bin_link, jnp.zeros((MOSTB,), jnp.int32)])
    nearby = lax.dynamic_slice(padded, (first,), (MOSTB,))
    lower = jnp.minimum(local_bin[:, None], local_bin[None, :])
    linked = jnp.zeros((group_slots, group_slots), jnp.int32)
    for height in range(MOSTB):
        linked = linked + jnp.where(lower == height, nearby[height], 0)
    spacing = jnp.abs(local_bin[:, None] - local_bin[None, :])
    paired = valid[:, None] & valid[None, :]
    allowed = paired & ((spacing == 0) | (spacing == 1) & (linked == 1))
    allowed = allowed | (position[:, None] == position[None, :])
    return allowed.astype(jnp.float32)


def contrast(query_rows, key_matrix, allowed, valid):
    similarity_scores = (
        lax.dot_general(
            query_rows, key_matrix, (((1,), (1,)), ((), ())), preferred_element_type=jnp.float32
        )
        / SOFTMAX_TEMP_SCALE
    )
    weights = allowed * jnp.exp(similarity_scores)
    shares = weights / jnp.sum(weights, axis=1, keepdims=True)
    position = jnp.arange(query_rows.shape[0], dtype=jnp.int32)
    diagonal = (position[:, None] == position[None, :]).astype(jnp.float32)
    logit_gradient = ((shares - diagonal) * valid[:, None]).astype(jnp.bfloat16)
    query_gradient = (
        jnp.dot(logit_gradient, key_matrix, preferred_element_type=jnp.float32) / SOFTMAX_TEMP_SCALE
    ).astype(jnp.bfloat16)
    key_gradient_rows = (
        lax.dot_general(
            logit_gradient, query_rows, (((0,), (0,)), ((), ())), preferred_element_type=jnp.float32
        )
        / SOFTMAX_TEMP_SCALE
    ).astype(jnp.bfloat16)
    return jnp.stack([query_gradient, key_gradient_rows], axis=1)


def dp_index():
    index = 0
    for name, size in DP_PARTS:
        index = index * size + lax.axis_index(name)
    return index


def local(features, head_weight, bin_of_row, bin_owner, bin_link):
    rows_dev, views, feat_dim = features.shape
    part_rows, emb_dim = head_weight.shape
    sources = 1
    for _, size in DP_PARTS:
        sources *= size
    bins_n = lax.axis_size("bin")
    bin_count = bin_owner.shape[0]
    per_bin = max(2, 2 * rows_dev // bin_count)
    per_owner = per_bin * MOSTB
    group_slots = sources * per_owner
    flat = features.reshape(rows_dev * views, feat_dim)
    folded = jnp.dot(
        flat,
        lax.all_gather(head_weight, "bin", axis=0, tiled=True),
        preferred_element_type=jnp.float32,
    )
    embedded = folded.reshape(rows_dev, views, emb_dim)
    scale = lax.rsqrt(jnp.sum(embedded * embedded, axis=2, keepdims=True) + 1e-06)
    unit = embedded * scale
    sent = unit.astype(jnp.bfloat16)
    row_bins = bin_of_row[:, 0]
    lookup = row_bins[:, None] == jnp.arange(bin_count, dtype=jnp.int32)[None, :]
    owner = jnp.sum(jnp.where(lookup, bin_owner[None, :], 0), axis=1)
    first_by_bin = jnp.sum((bin_owner[None, :] < bin_owner[:, None]).astype(jnp.int32), axis=1)
    local_bin = row_bins - jnp.sum(jnp.where(lookup, first_by_bin[None, :], 0), axis=1)
    order = jnp.arange(rows_dev, dtype=jnp.int32)
    earlier = (row_bins[:, None] == row_bins[None, :]) & (order[None, :] < order[:, None])
    seat = jnp.sum(earlier.astype(jnp.int32), axis=1)
    target = owner * per_owner + local_bin * per_bin + seat
    empty = jnp.zeros((group_slots, views, emb_dim), jnp.bfloat16).at[:, 0, 0].set(EMPTY_MARK)
    outbox = empty.at[target].set(sent)
    inbox = lax.all_to_all(
        outbox.reshape(sources, per_owner, views, emb_dim),
        DP,
        split_axis=0,
        concat_axis=0,
        tiled=True,
    )
    inbox = inbox.reshape(group_slots, views, emb_dim)
    valid = inbox[:, 0, 0] < 2.0
    inbox = jnp.where(valid[:, None, None], inbox, jnp.zeros_like(inbox))
    first = jnp.sum((bin_owner < dp_index()).astype(jnp.int32))
    allowed = allowed_mask(valid, first, bin_link, group_slots, per_bin)
    grads = contrast(inbox[:, 0], inbox[:, 1], allowed, valid.astype(jnp.float32))
    returned = lax.all_to_all(
        grads.reshape(sources, per_owner, views, emb_dim),
        DP,
        split_axis=0,
        concat_axis=0,
        tiled=True,
    )
    row_grads = returned.reshape(group_slots, views, emb_dim)[target].astype(jnp.float32)
    grad_rows = (
        scale * (row_grads - unit * jnp.sum(unit * row_grads, axis=2, keepdims=True))
    ).astype(jnp.bfloat16)
    column_start = lax.axis_index("bin") * part_rows
    trunk = lax.all_gather(features, "bin", axis=0, tiled=True)
    outgrad = lax.all_gather(grad_rows, "bin", axis=0, tiled=True)
    columns = lax.dynamic_slice_in_dim(trunk, column_start, part_rows, 2)
    count = trunk.shape[0]
    local_grad = lax.dot_general(
        columns.reshape(count * views, part_rows),
        outgrad.reshape(count * views, emb_dim),
        (((0,), (0,)), ((), ())),
        preferred_element_type=jnp.float32,
    )
    sizes = [size for _, size in DP_PARTS]
    per_dev = part_rows // sources
    local_grad = jnp.transpose(local_grad.reshape(*sizes, per_dev, emb_dim), (2, 0, 1, 3, 4))
    local_grad = lax.psum_scatter(
        local_grad.reshape(part_rows, emb_dim), "dc", scatter_dimension=0, tiled=True
    )
    planes = local_grad.reshape(sizes[0] * sizes[1], per_dev, emb_dim).astype(jnp.bfloat16)
    planes = lax.all_to_all(planes, ("dx", "dz"), split_axis=0, concat_axis=0, tiled=True)
    local_grad = jnp.sum(planes.astype(jnp.float32), axis=0)
    grad_weight = local_grad / rows_dev
    return (grad_rows, grad_weight)


def solution(mesh):
    sizes = [size for _, size in DP_PARTS]
    devices = mesh.devices.reshape(*sizes, mesh.devices.shape[1])
    parted = Mesh(devices, (*DP, "bin"))
    return jax.shard_map(
        local,
        mesh=parted,
        in_specs=(P((*DP, "bin"), None, None), P("bin", None), P((*DP, "bin"), None), P(), P()),
        out_specs=(P((*DP, "bin"), None, None), P(("bin", *DP), None)),
        check_vma=False,
    )
```

```python
import jax
import jax.numpy as jnp
from jax import lax
from jax.sharding import Mesh
from jax.sharding import PartitionSpec as P

MOSTB = 2


SOFTMAX_TEMP_SCALE = 0.1

DP_PARTS = (("dx", 4), ("dz", 16), ("dc", 2))
DP = tuple(name for name, _ in DP_PARTS)
EMPTY_MARK = 4.0


def allowed_mask(valid, first, bin_link, group_slots, per_bin):
    per_owner = per_bin * MOSTB
    position = jnp.arange(group_slots, dtype=jnp.int32)
    local_bin = position % per_owner // per_bin
    padded = jnp.concatenate([bin_link, jnp.zeros((MOSTB,), jnp.int32)])
    nearby = lax.dynamic_slice(padded, (first,), (MOSTB,))
    lower = jnp.minimum(local_bin[:, None], local_bin[None, :])
    linked = jnp.zeros((group_slots, group_slots), jnp.int32)
    for height in range(MOSTB):
        linked = linked + jnp.where(lower == height, nearby[height], 0)
    spacing = jnp.abs(local_bin[:, None] - local_bin[None, :])
    paired = valid[:, None] & valid[None, :]
    allowed = paired & ((spacing == 0) | (spacing == 1) & (linked == 1))
    allowed = allowed | (position[:, None] == position[None, :])
    return allowed.astype(jnp.float32)


def contrast(query_rows, key_matrix, allowed, valid):
    similarity_scores = (
        lax.dot_general(
            query_rows, key_matrix, (((1,), (1,)), ((), ())), preferred_element_type=jnp.float32
        )
        / SOFTMAX_TEMP_SCALE
    )
    weights = allowed * jnp.exp(similarity_scores)
    shares = weights / jnp.sum(weights, axis=1, keepdims=True)
    position = jnp.arange(query_rows.shape[0], dtype=jnp.int32)
    diagonal = (position[:, None] == position[None, :]).astype(jnp.float32)
    logit_gradient = ((shares - diagonal) * valid[:, None]).astype(jnp.bfloat16)
    query_gradient = (
        jnp.dot(logit_gradient, key_matrix, preferred_element_type=jnp.float32) / SOFTMAX_TEMP_SCALE
    ).astype(jnp.bfloat16)
    key_gradient_rows = (
        lax.dot_general(
            logit_gradient, query_rows, (((0,), (0,)), ((), ())), preferred_element_type=jnp.float32
        )
        / SOFTMAX_TEMP_SCALE
    ).astype(jnp.bfloat16)
    return jnp.stack([query_gradient, key_gradient_rows], axis=1)


def dp_index():
    index = 0
    for name, size in DP_PARTS:
        index = index * size + lax.axis_index(name)
    return index


def local(features, head_weight, bin_of_row, bin_owner, bin_link):
    rows_dev, views, feat_dim = features.shape
    part_rows, emb_dim = head_weight.shape
    sources = 1
    for _, size in DP_PARTS:
        sources *= size
    bins_n = lax.axis_size("bin")
    bin_count = bin_owner.shape[0]
    per_bin = max(2, 2 * rows_dev // bin_count)
    per_owner = per_bin * MOSTB
    group_slots = sources * per_owner
    flat = features.reshape(rows_dev * views, feat_dim)
    halves = head_weight.reshape(2, part_rows // 2, emb_dim)
    half = lax.dynamic_index_in_dim(halves, lax.axis_index("dc"), 0, keepdims=False)
    blocks = lax.all_gather(half, "bin", axis=0)
    blocks = lax.all_gather(blocks, "dc", axis=0)
    weight = jnp.transpose(blocks, (1, 0, 2, 3)).reshape(feat_dim, emb_dim)
    folded = jnp.dot(flat, weight, preferred_element_type=jnp.float32)
    embedded = folded.reshape(rows_dev, views, emb_dim)
    scale = lax.rsqrt(jnp.sum(embedded * embedded, axis=2, keepdims=True) + 1e-06)
    unit = embedded * scale
    sent = unit.astype(jnp.bfloat16)
    row_bins = bin_of_row[:, 0]
    lookup = row_bins[:, None] == jnp.arange(bin_count, dtype=jnp.int32)[None, :]
    owner = jnp.sum(jnp.where(lookup, bin_owner[None, :], 0), axis=1)
    first_by_bin = jnp.sum((bin_owner[None, :] < bin_owner[:, None]).astype(jnp.int32), axis=1)
    local_bin = row_bins - jnp.sum(jnp.where(lookup, first_by_bin[None, :], 0), axis=1)
    order = jnp.arange(rows_dev, dtype=jnp.int32)
    earlier = (row_bins[:, None] == row_bins[None, :]) & (order[None, :] < order[:, None])
    seat = jnp.sum(earlier.astype(jnp.int32), axis=1)
    target = owner * per_owner + local_bin * per_bin + seat
    empty = jnp.zeros((group_slots, views, emb_dim), jnp.bfloat16).at[:, 0, 0].set(EMPTY_MARK)
    outbox = empty.at[target].set(sent)
    inbox = lax.all_to_all(
        outbox.reshape(sources, per_owner, views, emb_dim),
        DP,
        split_axis=0,
        concat_axis=0,
        tiled=True,
    )
    inbox = inbox.reshape(group_slots, views, emb_dim)
    valid = inbox[:, 0, 0] < 2.0
    inbox = jnp.where(valid[:, None, None], inbox, jnp.zeros_like(inbox))
    first = jnp.sum((bin_owner < dp_index()).astype(jnp.int32))
    allowed = allowed_mask(valid, first, bin_link, group_slots, per_bin)
    grads = contrast(inbox[:, 0], inbox[:, 1], allowed, valid.astype(jnp.float32))
    returned = lax.all_to_all(
        grads.reshape(sources, per_owner, views, emb_dim),
        DP,
        split_axis=0,
        concat_axis=0,
        tiled=True,
    )
    row_grads = returned.reshape(group_slots, views, emb_dim)[target].astype(jnp.float32)
    grad_rows = (
        scale * (row_grads - unit * jnp.sum(unit * row_grads, axis=2, keepdims=True))
    ).astype(jnp.bfloat16)
    column_start = lax.axis_index("bin") * part_rows
    trunk = lax.all_gather(features, "bin", axis=0, tiled=True)
    outgrad = lax.all_gather(grad_rows, "bin", axis=0, tiled=True)
    columns = lax.dynamic_slice_in_dim(trunk, column_start, part_rows, 2)
    count = trunk.shape[0]
    local_grad = lax.dot_general(
        columns.reshape(count * views, part_rows),
        outgrad.reshape(count * views, emb_dim),
        (((0,), (0,)), ((), ())),
        preferred_element_type=jnp.float32,
    )
    sizes = [size for _, size in DP_PARTS]
    per_dev = part_rows // sources
    local_grad = jnp.transpose(local_grad.reshape(*sizes, per_dev, emb_dim), (2, 0, 1, 3, 4))
    local_grad = lax.psum_scatter(
        local_grad.reshape(part_rows, emb_dim), "dc", scatter_dimension=0, tiled=True
    )
    planes = local_grad.reshape(sizes[0] * sizes[1], per_dev, emb_dim).astype(jnp.bfloat16)
    planes = lax.all_to_all(planes, ("dx", "dz"), split_axis=0, concat_axis=0, tiled=True)
    local_grad = jnp.sum(planes.astype(jnp.float32), axis=0)
    grad_weight = local_grad / rows_dev
    return (grad_rows, grad_weight)


def solution(mesh):
    sizes = [size for _, size in DP_PARTS]
    devices = mesh.devices.reshape(*sizes, mesh.devices.shape[1])
    parted = Mesh(devices, (*DP, "bin"))
    return jax.shard_map(
        local,
        mesh=parted,
        in_specs=(P((*DP, "bin"), None, None), P("bin", None), P((*DP, "bin"), None), P(), P()),
        out_specs=(P((*DP, "bin"), None, None), P(("bin", *DP), None)),
        check_vma=False,
    )
```

```python
import jax
import jax.numpy as jnp
from jax import lax
from jax.sharding import Mesh
from jax.sharding import PartitionSpec as P

MOSTB = 2


SOFTMAX_TEMP_SCALE = 0.1

DP_PARTS = (("dx", 4), ("dz", 16), ("dc", 2))
DP = tuple(name for name, _ in DP_PARTS)
EMPTY_MARK = 4.0


def allowed_mask(valid, first, bin_link, group_slots, per_bin):
    per_owner = per_bin * MOSTB
    position = jnp.arange(group_slots, dtype=jnp.int32)
    local_bin = position % per_owner // per_bin
    padded = jnp.concatenate([bin_link, jnp.zeros((MOSTB,), jnp.int32)])
    nearby = lax.dynamic_slice(padded, (first,), (MOSTB,))
    lower = jnp.minimum(local_bin[:, None], local_bin[None, :])
    linked = jnp.zeros((group_slots, group_slots), jnp.int32)
    for height in range(MOSTB):
        linked = linked + jnp.where(lower == height, nearby[height], 0)
    spacing = jnp.abs(local_bin[:, None] - local_bin[None, :])
    paired = valid[:, None] & valid[None, :]
    allowed = paired & ((spacing == 0) | (spacing == 1) & (linked == 1))
    allowed = allowed | (position[:, None] == position[None, :])
    return allowed.astype(jnp.float32)


def contrast(query_rows, key_matrix, allowed, valid):
    similarity_scores = (
        lax.dot_general(
            query_rows, key_matrix, (((1,), (1,)), ((), ())), preferred_element_type=jnp.float32
        )
        / SOFTMAX_TEMP_SCALE
    )
    weights = allowed * jnp.exp(similarity_scores)
    shares = weights / jnp.sum(weights, axis=1, keepdims=True)
    position = jnp.arange(query_rows.shape[0], dtype=jnp.int32)
    diagonal = (position[:, None] == position[None, :]).astype(jnp.float32)
    logit_gradient = ((shares - diagonal) * valid[:, None]).astype(jnp.bfloat16)
    query_gradient = (
        jnp.dot(logit_gradient, key_matrix, preferred_element_type=jnp.float32) / SOFTMAX_TEMP_SCALE
    ).astype(jnp.bfloat16)
    key_gradient_rows = (
        lax.dot_general(
            logit_gradient, query_rows, (((0,), (0,)), ((), ())), preferred_element_type=jnp.float32
        )
        / SOFTMAX_TEMP_SCALE
    ).astype(jnp.bfloat16)
    return jnp.stack([query_gradient, key_gradient_rows], axis=1)


def dp_index():
    index = 0
    for name, size in DP_PARTS:
        index = index * size + lax.axis_index(name)
    return index


def local(features, head_weight, bin_of_row, bin_owner, bin_link):
    rows_dev, views, feat_dim = features.shape
    part_rows, emb_dim = head_weight.shape
    sources = 1
    for _, size in DP_PARTS:
        sources *= size
    bins_n = lax.axis_size("bin")
    bin_count = bin_owner.shape[0]
    per_bin = max(2, 2 * rows_dev // bin_count)
    per_owner = per_bin * MOSTB
    group_slots = sources * per_owner
    flat = features.reshape(rows_dev * views, feat_dim)
    copies = jnp.broadcast_to(head_weight[None], (bins_n, part_rows, emb_dim))
    weight = lax.all_to_all(copies, "bin", split_axis=0, concat_axis=0, tiled=True)
    weight = weight.reshape(feat_dim, emb_dim)
    folded = jnp.dot(flat, weight, preferred_element_type=jnp.float32)
    embedded = folded.reshape(rows_dev, views, emb_dim)
    scale = lax.rsqrt(jnp.sum(embedded * embedded, axis=2, keepdims=True) + 1e-06)
    unit = embedded * scale
    sent = unit.astype(jnp.bfloat16)
    row_bins = bin_of_row[:, 0]
    lookup = row_bins[:, None] == jnp.arange(bin_count, dtype=jnp.int32)[None, :]
    owner = jnp.sum(jnp.where(lookup, bin_owner[None, :], 0), axis=1)
    first_by_bin = jnp.sum((bin_owner[None, :] < bin_owner[:, None]).astype(jnp.int32), axis=1)
    local_bin = row_bins - jnp.sum(jnp.where(lookup, first_by_bin[None, :], 0), axis=1)
    order = jnp.arange(rows_dev, dtype=jnp.int32)
    earlier = (row_bins[:, None] == row_bins[None, :]) & (order[None, :] < order[:, None])
    seat = jnp.sum(earlier.astype(jnp.int32), axis=1)
    target = owner * per_owner + local_bin * per_bin + seat
    empty = jnp.zeros((group_slots, views, emb_dim), jnp.bfloat16).at[:, 0, 0].set(EMPTY_MARK)
    outbox = empty.at[target].set(sent)
    inbox = lax.all_to_all(
        outbox.reshape(sources, per_owner, views, emb_dim),
        DP,
        split_axis=0,
        concat_axis=0,
        tiled=True,
    )
    inbox = inbox.reshape(group_slots, views, emb_dim)
    valid = inbox[:, 0, 0] < 2.0
    inbox = jnp.where(valid[:, None, None], inbox, jnp.zeros_like(inbox))
    first = jnp.sum((bin_owner < dp_index()).astype(jnp.int32))
    allowed = allowed_mask(valid, first, bin_link, group_slots, per_bin)
    grads = contrast(inbox[:, 0], inbox[:, 1], allowed, valid.astype(jnp.float32))
    returned = lax.all_to_all(
        grads.reshape(sources, per_owner, views, emb_dim),
        DP,
        split_axis=0,
        concat_axis=0,
        tiled=True,
    )
    row_grads = returned.reshape(group_slots, views, emb_dim)[target].astype(jnp.float32)
    grad_rows = (
        scale * (row_grads - unit * jnp.sum(unit * row_grads, axis=2, keepdims=True))
    ).astype(jnp.bfloat16)
    column_start = lax.axis_index("bin") * part_rows
    trunk = lax.all_gather(features, "bin", axis=0, tiled=True)
    outgrad = lax.all_gather(grad_rows, "bin", axis=0, tiled=True)
    columns = lax.dynamic_slice_in_dim(trunk, column_start, part_rows, 2)
    count = trunk.shape[0]
    local_grad = lax.dot_general(
        columns.reshape(count * views, part_rows),
        outgrad.reshape(count * views, emb_dim),
        (((0,), (0,)), ((), ())),
        preferred_element_type=jnp.float32,
    )
    sizes = [size for _, size in DP_PARTS]
    per_dev = part_rows // sources
    local_grad = jnp.transpose(local_grad.reshape(*sizes, per_dev, emb_dim), (2, 0, 1, 3, 4))
    local_grad = lax.psum_scatter(
        local_grad.reshape(part_rows, emb_dim), "dc", scatter_dimension=0, tiled=True
    )
    planes = local_grad.reshape(sizes[0] * sizes[1], per_dev, emb_dim).astype(jnp.bfloat16)
    planes = lax.all_to_all(planes, ("dx", "dz"), split_axis=0, concat_axis=0, tiled=True)
    local_grad = jnp.sum(planes.astype(jnp.float32), axis=0)
    grad_weight = local_grad / rows_dev
    return (grad_rows, grad_weight)


def solution(mesh):
    sizes = [size for _, size in DP_PARTS]
    devices = mesh.devices.reshape(*sizes, mesh.devices.shape[1])
    parted = Mesh(devices, (*DP, "bin"))
    return jax.shard_map(
        local,
        mesh=parted,
        in_specs=(P((*DP, "bin"), None, None), P("bin", None), P((*DP, "bin"), None), P(), P()),
        out_specs=(P((*DP, "bin"), None, None), P(("bin", *DP), None)),
        check_vma=False,
    )
```

```python
import jax
import jax.numpy as jnp
from jax import lax
from jax.sharding import Mesh
from jax.sharding import PartitionSpec as P

MOSTB = 2


SOFTMAX_TEMP_SCALE = 0.1

DP_PARTS = (("dx", 4), ("dz", 16), ("dc", 2))
DP = tuple(name for name, _ in DP_PARTS)
EMPTY_MARK = 4.0


def allowed_mask(valid, first, bin_link, group_slots, per_bin):
    per_owner = per_bin * MOSTB
    position = jnp.arange(group_slots, dtype=jnp.int32)
    local_bin = position % per_owner // per_bin
    padded = jnp.concatenate([bin_link, jnp.zeros((MOSTB,), jnp.int32)])
    nearby = lax.dynamic_slice(padded, (first,), (MOSTB,))
    lower = jnp.minimum(local_bin[:, None], local_bin[None, :])
    linked = jnp.zeros((group_slots, group_slots), jnp.int32)
    for height in range(MOSTB):
        linked = linked + jnp.where(lower == height, nearby[height], 0)
    spacing = jnp.abs(local_bin[:, None] - local_bin[None, :])
    paired = valid[:, None] & valid[None, :]
    allowed = paired & ((spacing == 0) | (spacing == 1) & (linked == 1))
    allowed = allowed | (position[:, None] == position[None, :])
    return allowed.astype(jnp.float32)


def contrast(query_rows, key_matrix, allowed, valid):
    similarity_scores = (
        lax.dot_general(
            query_rows, key_matrix, (((1,), (1,)), ((), ())), preferred_element_type=jnp.float32
        )
        / SOFTMAX_TEMP_SCALE
    )
    weights = allowed * jnp.exp(similarity_scores)
    shares = weights / jnp.sum(weights, axis=1, keepdims=True)
    position = jnp.arange(query_rows.shape[0], dtype=jnp.int32)
    diagonal = (position[:, None] == position[None, :]).astype(jnp.float32)
    logit_gradient = ((shares - diagonal) * valid[:, None]).astype(jnp.bfloat16)
    query_gradient = (
        jnp.dot(logit_gradient, key_matrix, preferred_element_type=jnp.float32) / SOFTMAX_TEMP_SCALE
    ).astype(jnp.bfloat16)
    key_gradient_rows = (
        lax.dot_general(
            logit_gradient, query_rows, (((0,), (0,)), ((), ())), preferred_element_type=jnp.float32
        )
        / SOFTMAX_TEMP_SCALE
    ).astype(jnp.bfloat16)
    return query_gradient, key_gradient_rows


def dp_index():
    index = 0
    for name, size in DP_PARTS:
        index = index * size + lax.axis_index(name)
    return index


def local(features, head_weight, bin_of_row, bin_owner, bin_link):
    rows_dev, views, feat_dim = features.shape
    part_rows, emb_dim = head_weight.shape
    sources = 1
    for _, size in DP_PARTS:
        sources *= size
    bins_n = lax.axis_size("bin")
    bin_count = bin_owner.shape[0]
    per_bin = max(2, 2 * rows_dev // bin_count)
    per_owner = per_bin * MOSTB
    group_slots = sources * per_owner
    flat = features.reshape(rows_dev * views, feat_dim)
    copies = jnp.broadcast_to(head_weight[None], (bins_n, part_rows, emb_dim))
    weight = lax.all_to_all(copies, "bin", split_axis=0, concat_axis=0, tiled=True)
    weight = weight.reshape(feat_dim, emb_dim)
    folded = jnp.dot(flat, weight, preferred_element_type=jnp.float32)
    embedded = folded.reshape(rows_dev, views, emb_dim)
    scale = lax.rsqrt(jnp.sum(embedded * embedded, axis=2, keepdims=True) + 1e-06)
    unit = embedded * scale
    sent = unit.astype(jnp.bfloat16)
    row_bins = bin_of_row[:, 0]
    lookup = row_bins[:, None] == jnp.arange(bin_count, dtype=jnp.int32)[None, :]
    owner = jnp.sum(jnp.where(lookup, bin_owner[None, :], 0), axis=1)
    first_by_bin = jnp.sum((bin_owner[None, :] < bin_owner[:, None]).astype(jnp.int32), axis=1)
    local_bin = row_bins - jnp.sum(jnp.where(lookup, first_by_bin[None, :], 0), axis=1)
    order = jnp.arange(rows_dev, dtype=jnp.int32)
    earlier = (row_bins[:, None] == row_bins[None, :]) & (order[None, :] < order[:, None])
    seat = jnp.sum(earlier.astype(jnp.int32), axis=1)
    target = owner * per_owner + local_bin * per_bin + seat
    empty = jnp.zeros((group_slots, views, emb_dim), jnp.bfloat16).at[:, 0, 0].set(EMPTY_MARK)
    outbox = empty.at[target].set(sent)
    inbox = lax.all_to_all(
        outbox.reshape(sources, per_owner, views, emb_dim),
        DP,
        split_axis=0,
        concat_axis=0,
        tiled=True,
    )
    inbox = inbox.reshape(group_slots, views, emb_dim)
    trunks = [lax.all_gather(features[:, view], "bin", axis=0, tiled=True) for view in range(views)]
    inbox, trunks = lax.optimization_barrier((inbox, trunks))
    valid = inbox[:, 0, 0] < 2.0
    inbox = jnp.where(valid[:, None, None], inbox, jnp.zeros_like(inbox))
    first = jnp.sum((bin_owner < dp_index()).astype(jnp.int32))
    allowed = allowed_mask(valid, first, bin_link, group_slots, per_bin)
    grads = contrast(inbox[:, 0], inbox[:, 1], allowed, valid.astype(jnp.float32))
    column_start = lax.axis_index("bin") * part_rows
    view_rows = []
    local_grad = None
    for view, view_grads in enumerate(grads):
        if view_rows:
            view_grads, _ = lax.optimization_barrier((view_grads, view_rows[-1]))
        returned = lax.all_to_all(
            view_grads.reshape(sources, per_owner, emb_dim),
            DP,
            split_axis=0,
            concat_axis=0,
            tiled=True,
        )
        row_grads = returned.reshape(group_slots, emb_dim)[target].astype(jnp.float32)
        view_unit = unit[:, view]
        projected = row_grads - view_unit * jnp.sum(view_unit * row_grads, axis=1, keepdims=True)
        rows_out = (scale[:, view] * projected).astype(jnp.bfloat16)
        view_rows.append(rows_out)
        columns = lax.dynamic_slice_in_dim(trunks[view], column_start, part_rows, 1)
        outgrad = lax.all_gather(rows_out, "bin", axis=0, tiled=True)
        term = lax.dot_general(
            columns, outgrad, (((0,), (0,)), ((), ())), preferred_element_type=jnp.float32
        )
        local_grad = term if local_grad is None else local_grad + term
    grad_rows = jnp.stack(view_rows, axis=1)
    sizes = [size for _, size in DP_PARTS]
    per_dev = part_rows // sources
    local_grad = jnp.transpose(local_grad.reshape(*sizes, per_dev, emb_dim), (2, 0, 1, 3, 4))
    local_grad = lax.psum_scatter(
        local_grad.reshape(part_rows, emb_dim).astype(jnp.bfloat16), "dc", scatter_dimension=0, tiled=True
    )
    planes = local_grad.reshape(sizes[0] * sizes[1], per_dev, emb_dim)
    planes = lax.all_to_all(planes, ("dx", "dz"), split_axis=0, concat_axis=0, tiled=True)
    local_grad = jnp.sum(planes.astype(jnp.float32), axis=0)
    grad_weight = local_grad / rows_dev
    return (grad_rows, grad_weight)


def solution(mesh):
    sizes = [size for _, size in DP_PARTS]
    devices = mesh.devices.reshape(*sizes, mesh.devices.shape[1])
    parted = Mesh(devices, (*DP, "bin"))
    return jax.shard_map(
        local,
        mesh=parted,
        in_specs=(P((*DP, "bin"), None, None), P("bin", None), P((*DP, "bin"), None), P(), P()),
        out_specs=(P((*DP, "bin"), None, None), P(("bin", *DP), None)),
        check_vma=False,
    )
```

```python
import jax
import jax.numpy as jnp
from jax import lax
from jax.sharding import Mesh
from jax.sharding import PartitionSpec as P

MOSTB = 2


SOFTMAX_TEMP_SCALE = 0.1

DP_PARTS = (("dx", 4), ("dz", 16), ("dc", 2))
DP = tuple(name for name, _ in DP_PARTS)
EMPTY_MARK = 4.0


def allowed_mask(valid, first, bin_link, group_slots, per_bin):
    per_owner = per_bin * MOSTB
    position = jnp.arange(group_slots, dtype=jnp.int32)
    local_bin = position % per_owner // per_bin
    padded = jnp.concatenate([bin_link, jnp.zeros((MOSTB,), jnp.int32)])
    nearby = lax.dynamic_slice(padded, (first,), (MOSTB,))
    lower = jnp.minimum(local_bin[:, None], local_bin[None, :])
    linked = jnp.zeros((group_slots, group_slots), jnp.int32)
    for height in range(MOSTB):
        linked = linked + jnp.where(lower == height, nearby[height], 0)
    spacing = jnp.abs(local_bin[:, None] - local_bin[None, :])
    paired = valid[:, None] & valid[None, :]
    allowed = paired & ((spacing == 0) | (spacing == 1) & (linked == 1))
    allowed = allowed | (position[:, None] == position[None, :])
    return allowed.astype(jnp.float32)


def contrast(query_rows, key_matrix, allowed, valid):
    similarity_scores = (
        lax.dot_general(
            query_rows, key_matrix, (((1,), (1,)), ((), ())), preferred_element_type=jnp.float32
        )
        / SOFTMAX_TEMP_SCALE
    )
    weights = allowed * jnp.exp(similarity_scores)
    shares = weights / jnp.sum(weights, axis=1, keepdims=True)
    position = jnp.arange(query_rows.shape[0], dtype=jnp.int32)
    diagonal = (position[:, None] == position[None, :]).astype(jnp.float32)
    logit_gradient = ((shares - diagonal) * valid[:, None]).astype(jnp.bfloat16)
    query_gradient = (
        jnp.dot(logit_gradient, key_matrix, preferred_element_type=jnp.float32) / SOFTMAX_TEMP_SCALE
    ).astype(jnp.bfloat16)
    key_gradient_rows = (
        lax.dot_general(
            logit_gradient, query_rows, (((0,), (0,)), ((), ())), preferred_element_type=jnp.float32
        )
        / SOFTMAX_TEMP_SCALE
    ).astype(jnp.bfloat16)
    return jnp.stack([query_gradient, key_gradient_rows], axis=1)


def dp_index():
    index = 0
    for name, size in DP_PARTS:
        index = index * size + lax.axis_index(name)
    return index


def local(features, head_weight, bin_of_row, bin_owner, bin_link):
    rows_dev, views, feat_dim = features.shape
    part_rows, emb_dim = head_weight.shape
    sources = 1
    for _, size in DP_PARTS:
        sources *= size
    bins_n = lax.axis_size("bin")
    bin_count = bin_owner.shape[0]
    per_bin = max(2, 2 * rows_dev // bin_count)
    per_owner = per_bin * MOSTB
    group_slots = sources * per_owner
    flat = features.reshape(rows_dev * views, feat_dim)
    core = lax.axis_index("dc")
    halves = head_weight.reshape(2, part_rows // 2, emb_dim)
    half = lax.dynamic_index_in_dim(halves, core, 0, keepdims=False)
    copies = jnp.broadcast_to(half[None], (bins_n, part_rows // 2, emb_dim))
    mine = lax.all_to_all(copies, "bin", split_axis=0, concat_axis=0, tiled=True)
    theirs = lax.ppermute(mine, "dc", perm=[(0, 1), (1, 0)])
    low = jnp.where(core == 0, mine, theirs)
    high = jnp.where(core == 0, theirs, mine)
    weight = jnp.stack([low, high], axis=1).reshape(feat_dim, emb_dim)
    folded = jnp.dot(flat, weight, preferred_element_type=jnp.float32)
    embedded = folded.reshape(rows_dev, views, emb_dim)
    scale = lax.rsqrt(jnp.sum(embedded * embedded, axis=2, keepdims=True) + 1e-06)
    unit = embedded * scale
    sent = unit.astype(jnp.bfloat16)
    row_bins = bin_of_row[:, 0]
    lookup = row_bins[:, None] == jnp.arange(bin_count, dtype=jnp.int32)[None, :]
    owner = jnp.sum(jnp.where(lookup, bin_owner[None, :], 0), axis=1)
    first_by_bin = jnp.sum((bin_owner[None, :] < bin_owner[:, None]).astype(jnp.int32), axis=1)
    local_bin = row_bins - jnp.sum(jnp.where(lookup, first_by_bin[None, :], 0), axis=1)
    order = jnp.arange(rows_dev, dtype=jnp.int32)
    earlier = (row_bins[:, None] == row_bins[None, :]) & (order[None, :] < order[:, None])
    seat = jnp.sum(earlier.astype(jnp.int32), axis=1)
    target = owner * per_owner + local_bin * per_bin + seat
    empty = jnp.zeros((group_slots, views, emb_dim), jnp.bfloat16).at[:, 0, 0].set(EMPTY_MARK)
    outbox = empty.at[target].set(sent)
    inbox = lax.all_to_all(
        outbox.reshape(sources, per_owner, views, emb_dim),
        DP,
        split_axis=0,
        concat_axis=0,
        tiled=True,
    )
    inbox = inbox.reshape(group_slots, views, emb_dim)
    valid = inbox[:, 0, 0] < 2.0
    inbox = jnp.where(valid[:, None, None], inbox, jnp.zeros_like(inbox))
    first = jnp.sum((bin_owner < dp_index()).astype(jnp.int32))
    allowed = allowed_mask(valid, first, bin_link, group_slots, per_bin)
    grads = contrast(inbox[:, 0], inbox[:, 1], allowed, valid.astype(jnp.float32))
    returned = lax.all_to_all(
        grads.reshape(sources, per_owner, views, emb_dim),
        DP,
        split_axis=0,
        concat_axis=0,
        tiled=True,
    )
    row_grads = returned.reshape(group_slots, views, emb_dim)[target].astype(jnp.float32)
    grad_rows = (
        scale * (row_grads - unit * jnp.sum(unit * row_grads, axis=2, keepdims=True))
    ).astype(jnp.bfloat16)
    column_start = lax.axis_index("bin") * part_rows
    trunk = lax.all_gather(features, "bin", axis=0, tiled=True)
    outgrad = lax.all_gather(grad_rows, "bin", axis=0, tiled=True)
    columns = lax.dynamic_slice_in_dim(trunk, column_start, part_rows, 2)
    count = trunk.shape[0]
    local_grad = lax.dot_general(
        columns.reshape(count * views, part_rows),
        outgrad.reshape(count * views, emb_dim),
        (((0,), (0,)), ((), ())),
        preferred_element_type=jnp.float32,
    )
    sizes = [size for _, size in DP_PARTS]
    per_dev = part_rows // sources
    local_grad = jnp.transpose(local_grad.reshape(*sizes, per_dev, emb_dim), (2, 0, 1, 3, 4))
    local_grad = lax.psum_scatter(
        local_grad.reshape(part_rows, emb_dim), "dc", scatter_dimension=0, tiled=True
    )
    planes = local_grad.reshape(sizes[0] * sizes[1], per_dev, emb_dim).astype(jnp.bfloat16)
    planes = lax.all_to_all(planes, ("dx", "dz"), split_axis=0, concat_axis=0, tiled=True)
    local_grad = jnp.sum(planes.astype(jnp.float32), axis=0)
    grad_weight = local_grad / rows_dev
    return (grad_rows, grad_weight)


def solution(mesh):
    sizes = [size for _, size in DP_PARTS]
    devices = mesh.devices.reshape(*sizes, mesh.devices.shape[1])
    parted = Mesh(devices, (*DP, "bin"))
    return jax.shard_map(
        local,
        mesh=parted,
        in_specs=(P((*DP, "bin"), None, None), P("bin", None), P((*DP, "bin"), None), P(), P()),
        out_specs=(P((*DP, "bin"), None, None), P(("bin", *DP), None)),
        check_vma=False,
    )
```

```python
import jax
import jax.numpy as jnp
from jax import lax
from jax.sharding import Mesh
from jax.sharding import PartitionSpec as P

MOSTB = 2


SOFTMAX_TEMP_SCALE = 0.1

DP_PARTS = (("dx", 4), ("dz", 16), ("dc", 2))
DP = tuple(name for name, _ in DP_PARTS)
EMPTY_MARK = 4.0


def allowed_mask(valid, first, bin_link, group_slots, per_bin):
    per_owner = per_bin * MOSTB
    position = jnp.arange(group_slots, dtype=jnp.int32)
    local_bin = position % per_owner // per_bin
    padded = jnp.concatenate([bin_link, jnp.zeros((MOSTB,), jnp.int32)])
    nearby = lax.dynamic_slice(padded, (first,), (MOSTB,))
    lower = jnp.minimum(local_bin[:, None], local_bin[None, :])
    linked = jnp.zeros((group_slots, group_slots), jnp.int32)
    for height in range(MOSTB):
        linked = linked + jnp.where(lower == height, nearby[height], 0)
    spacing = jnp.abs(local_bin[:, None] - local_bin[None, :])
    paired = valid[:, None] & valid[None, :]
    allowed = paired & ((spacing == 0) | (spacing == 1) & (linked == 1))
    allowed = allowed | (position[:, None] == position[None, :])
    return allowed.astype(jnp.float32)


def contrast(query_rows, key_matrix, allowed, valid):
    similarity_scores = (
        lax.dot_general(
            query_rows, key_matrix, (((1,), (1,)), ((), ())), preferred_element_type=jnp.float32
        )
        / SOFTMAX_TEMP_SCALE
    )
    weights = allowed * jnp.exp(similarity_scores)
    shares = weights / jnp.sum(weights, axis=1, keepdims=True)
    position = jnp.arange(query_rows.shape[0], dtype=jnp.int32)
    diagonal = (position[:, None] == position[None, :]).astype(jnp.float32)
    logit_gradient = ((shares - diagonal) * valid[:, None]).astype(jnp.bfloat16)
    query_gradient = (
        jnp.dot(logit_gradient, key_matrix, preferred_element_type=jnp.float32) / SOFTMAX_TEMP_SCALE
    ).astype(jnp.bfloat16)
    key_gradient_rows = (
        lax.dot_general(
            logit_gradient, query_rows, (((0,), (0,)), ((), ())), preferred_element_type=jnp.float32
        )
        / SOFTMAX_TEMP_SCALE
    ).astype(jnp.bfloat16)
    return jnp.stack([query_gradient, key_gradient_rows], axis=1)


def dp_index():
    index = 0
    for name, size in DP_PARTS:
        index = index * size + lax.axis_index(name)
    return index


def local(features, head_weight, bin_of_row, bin_owner, bin_link):
    rows_dev, views, feat_dim = features.shape
    part_rows, emb_dim = head_weight.shape
    sources = 1
    for _, size in DP_PARTS:
        sources *= size
    bins_n = lax.axis_size("bin")
    bin_count = bin_owner.shape[0]
    per_bin = max(2, 2 * rows_dev // bin_count)
    per_owner = per_bin * MOSTB
    group_slots = sources * per_owner
    flat = features.reshape(rows_dev * views, feat_dim)
    core = lax.axis_index("dc")
    halves = head_weight.reshape(2, part_rows // 2, emb_dim)
    half = lax.dynamic_index_in_dim(halves, core, 0, keepdims=False)
    copies = jnp.broadcast_to(half[None], (bins_n, part_rows // 2, emb_dim))
    mine = lax.all_to_all(copies, "bin", split_axis=0, concat_axis=0, tiled=True)
    theirs = lax.ppermute(mine, "dc", perm=[(0, 1), (1, 0)])
    low = jnp.where(core == 0, mine, theirs)
    high = jnp.where(core == 0, theirs, mine)
    weight = jnp.stack([low, high], axis=1).reshape(feat_dim, emb_dim)
    folded = jnp.dot(flat, weight, preferred_element_type=jnp.float32)
    embedded = folded.reshape(rows_dev, views, emb_dim)
    scale = lax.rsqrt(jnp.sum(embedded * embedded, axis=2, keepdims=True) + 1e-06)
    unit = embedded * scale
    sent = unit.astype(jnp.bfloat16)
    row_bins = bin_of_row[:, 0]
    lookup = row_bins[:, None] == jnp.arange(bin_count, dtype=jnp.int32)[None, :]
    owner = jnp.sum(jnp.where(lookup, bin_owner[None, :], 0), axis=1)
    first_by_bin = jnp.sum((bin_owner[None, :] < bin_owner[:, None]).astype(jnp.int32), axis=1)
    local_bin = row_bins - jnp.sum(jnp.where(lookup, first_by_bin[None, :], 0), axis=1)
    order = jnp.arange(rows_dev, dtype=jnp.int32)
    earlier = (row_bins[:, None] == row_bins[None, :]) & (order[None, :] < order[:, None])
    seat = jnp.sum(earlier.astype(jnp.int32), axis=1)
    target = owner * per_owner + local_bin * per_bin + seat
    picks = target[None, :] == jnp.arange(group_slots, dtype=jnp.int32)[:, None]
    picked = jnp.dot(
        picks.astype(jnp.bfloat16),
        sent.reshape(rows_dev, views * emb_dim),
        preferred_element_type=jnp.float32,
    ).reshape(group_slots, views, emb_dim)
    unfilled = 1.0 - jnp.any(picks, axis=1).astype(jnp.float32)
    mark = jnp.zeros((views, emb_dim), jnp.float32).at[0, 0].set(EMPTY_MARK)
    outbox = (picked + unfilled[:, None, None] * mark[None]).astype(jnp.bfloat16)
    inbox = lax.all_to_all(
        outbox.reshape(sources, per_owner, views, emb_dim),
        DP,
        split_axis=0,
        concat_axis=0,
        tiled=True,
    )
    inbox = inbox.reshape(group_slots, views, emb_dim)
    valid = inbox[:, 0, 0] < 2.0
    inbox = jnp.where(valid[:, None, None], inbox, jnp.zeros_like(inbox))
    first = jnp.sum((bin_owner < dp_index()).astype(jnp.int32))
    allowed = allowed_mask(valid, first, bin_link, group_slots, per_bin)
    grads = contrast(inbox[:, 0], inbox[:, 1], allowed, valid.astype(jnp.float32))
    returned = lax.all_to_all(
        grads.reshape(sources, per_owner, views, emb_dim),
        DP,
        split_axis=0,
        concat_axis=0,
        tiled=True,
    )
    row_grads = lax.dot_general(
        picks.astype(jnp.bfloat16),
        returned.reshape(group_slots, views * emb_dim),
        (((0,), (0,)), ((), ())),
        preferred_element_type=jnp.float32,
    ).reshape(rows_dev, views, emb_dim)
    grad_rows = (
        scale * (row_grads - unit * jnp.sum(unit * row_grads, axis=2, keepdims=True))
    ).astype(jnp.bfloat16)
    column_start = lax.axis_index("bin") * part_rows
    trunk = lax.all_gather(features, "bin", axis=0, tiled=True)
    outgrad = lax.all_to_all(
        jnp.broadcast_to(grad_rows[None], (bins_n, *grad_rows.shape)),
        "bin",
        split_axis=0,
        concat_axis=0,
        tiled=True,
    )
    columns = lax.dynamic_slice_in_dim(trunk, column_start, part_rows, 2)
    count = trunk.shape[0]
    local_grad = lax.dot_general(
        columns.reshape(count * views, part_rows),
        outgrad.reshape(count * views, emb_dim),
        (((0,), (0,)), ((), ())),
        preferred_element_type=jnp.float32,
    )
    sizes = [size for _, size in DP_PARTS]
    per_dev = part_rows // sources
    local_grad = jnp.transpose(local_grad.reshape(*sizes, per_dev, emb_dim), (2, 0, 1, 3, 4))
    kept = lax.dynamic_index_in_dim(local_grad, core, 0, keepdims=False)
    given = lax.dynamic_index_in_dim(local_grad, 1 - core, 0, keepdims=False)
    local_grad = kept + lax.ppermute(given, "dc", perm=[(0, 1), (1, 0)])
    planes = local_grad.reshape(sizes[0] * sizes[1], per_dev, emb_dim).astype(jnp.bfloat16)
    planes = lax.all_to_all(planes, ("dx", "dz"), split_axis=0, concat_axis=0, tiled=True)
    local_grad = jnp.sum(planes.astype(jnp.float32), axis=0)
    grad_weight = local_grad / rows_dev
    return (grad_rows, grad_weight)


def solution(mesh):
    sizes = [size for _, size in DP_PARTS]
    devices = mesh.devices.reshape(*sizes, mesh.devices.shape[1])
    parted = Mesh(devices, (*DP, "bin"))
    return jax.shard_map(
        local,
        mesh=parted,
        in_specs=(P((*DP, "bin"), None, None), P("bin", None), P((*DP, "bin"), None), P(), P()),
        out_specs=(P((*DP, "bin"), None, None), P(("bin", *DP), None)),
        check_vma=False,
    )
```

```python
import jax
import jax.numpy as jnp
from jax import lax
from jax.sharding import Mesh
from jax.sharding import PartitionSpec as P

MOSTB = 2


SOFTMAX_TEMP_SCALE = 0.1

DP_PARTS = (("dx", 4), ("dz", 16), ("dc", 2))
DP = tuple(name for name, _ in DP_PARTS)
EMPTY_MARK = 4.0


def allowed_mask(valid, first, bin_link, group_slots, per_bin):
    per_owner = per_bin * MOSTB
    position = jnp.arange(group_slots, dtype=jnp.int32)
    local_bin = position % per_owner // per_bin
    padded = jnp.concatenate([bin_link, jnp.zeros((MOSTB,), jnp.int32)])
    nearby = lax.dynamic_slice(padded, (first,), (MOSTB,))
    lower = jnp.minimum(local_bin[:, None], local_bin[None, :])
    linked = jnp.zeros((group_slots, group_slots), jnp.int32)
    for height in range(MOSTB):
        linked = linked + jnp.where(lower == height, nearby[height], 0)
    spacing = jnp.abs(local_bin[:, None] - local_bin[None, :])
    paired = valid[:, None] & valid[None, :]
    allowed = paired & ((spacing == 0) | (spacing == 1) & (linked == 1))
    allowed = allowed | (position[:, None] == position[None, :])
    return allowed.astype(jnp.float32)


def contrast(query_rows, key_matrix, allowed, valid):
    similarity_scores = (
        lax.dot_general(
            query_rows, key_matrix, (((1,), (1,)), ((), ())), preferred_element_type=jnp.float32
        )
        / SOFTMAX_TEMP_SCALE
    )
    weights = allowed * jnp.exp(similarity_scores)
    shares = weights / jnp.sum(weights, axis=1, keepdims=True)
    position = jnp.arange(query_rows.shape[0], dtype=jnp.int32)
    diagonal = (position[:, None] == position[None, :]).astype(jnp.float32)
    logit_gradient = ((shares - diagonal) * valid[:, None]).astype(jnp.bfloat16)
    query_gradient = (
        jnp.dot(logit_gradient, key_matrix, preferred_element_type=jnp.float32) / SOFTMAX_TEMP_SCALE
    ).astype(jnp.bfloat16)
    key_gradient_rows = (
        lax.dot_general(
            logit_gradient, query_rows, (((0,), (0,)), ((), ())), preferred_element_type=jnp.float32
        )
        / SOFTMAX_TEMP_SCALE
    ).astype(jnp.bfloat16)
    return query_gradient, key_gradient_rows


def dp_index():
    index = 0
    for name, size in DP_PARTS:
        index = index * size + lax.axis_index(name)
    return index


def local(features, head_weight, bin_of_row, bin_owner, bin_link):
    rows_dev, views, feat_dim = features.shape
    part_rows, emb_dim = head_weight.shape
    sources = 1
    for _, size in DP_PARTS:
        sources *= size
    bins_n = lax.axis_size("bin")
    bin_count = bin_owner.shape[0]
    per_bin = max(2, 2 * rows_dev // bin_count)
    per_owner = per_bin * MOSTB
    group_slots = sources * per_owner
    flat = features.reshape(rows_dev * views, feat_dim)
    core = lax.axis_index("dc")
    halves = head_weight.reshape(2, part_rows // 2, emb_dim)
    half = lax.dynamic_index_in_dim(halves, core, 0, keepdims=False)
    copies = jnp.broadcast_to(half[None], (bins_n, part_rows // 2, emb_dim))
    mine = lax.all_to_all(copies, "bin", split_axis=0, concat_axis=0, tiled=True)
    theirs = lax.ppermute(mine, "dc", perm=[(0, 1), (1, 0)])
    low = jnp.where(core == 0, mine, theirs)
    high = jnp.where(core == 0, theirs, mine)
    weight = jnp.stack([low, high], axis=1).reshape(feat_dim, emb_dim)
    folded = jnp.dot(flat, weight, preferred_element_type=jnp.float32)
    embedded = folded.reshape(rows_dev, views, emb_dim)
    scale = lax.rsqrt(jnp.sum(embedded * embedded, axis=2, keepdims=True) + 1e-06)
    unit = embedded * scale
    sent = unit.astype(jnp.bfloat16)
    row_bins = bin_of_row[:, 0]
    lookup = row_bins[:, None] == jnp.arange(bin_count, dtype=jnp.int32)[None, :]
    owner = jnp.sum(jnp.where(lookup, bin_owner[None, :], 0), axis=1)
    first_by_bin = jnp.sum((bin_owner[None, :] < bin_owner[:, None]).astype(jnp.int32), axis=1)
    local_bin = row_bins - jnp.sum(jnp.where(lookup, first_by_bin[None, :], 0), axis=1)
    order = jnp.arange(rows_dev, dtype=jnp.int32)
    earlier = (row_bins[:, None] == row_bins[None, :]) & (order[None, :] < order[:, None])
    seat = jnp.sum(earlier.astype(jnp.int32), axis=1)
    target = owner * per_owner + local_bin * per_bin + seat
    block = views * per_owner
    dest = (
        (target // per_owner)[:, None] * block
        + jnp.arange(views, dtype=jnp.int32)[None, :] * per_owner
        + (target % per_owner)[:, None]
    )
    lanes = sources * block
    picks = (dest.reshape(-1)[None, :] == jnp.arange(lanes, dtype=jnp.int32)[:, None]).astype(jnp.bfloat16)
    picked = jnp.dot(
        picks, sent.reshape(rows_dev * views, emb_dim), preferred_element_type=jnp.float32
    )
    unfilled = 1.0 - jnp.sum(picks.astype(jnp.float32), axis=1)
    first_lane = (jnp.arange(emb_dim, dtype=jnp.int32) == 0).astype(jnp.float32)
    outbox = (picked + (unfilled * EMPTY_MARK)[:, None] * first_lane[None, :]).astype(jnp.bfloat16)
    inbox = lax.all_to_all(
        outbox.reshape(sources, block, emb_dim), DP, split_axis=0, concat_axis=0, tiled=True
    )
    inbox = inbox.reshape(sources, views, per_owner, emb_dim)
    valid = (inbox[:, 0, :, 0] < 2.0).reshape(group_slots)
    query = jnp.where(valid[:, None], inbox[:, 0].reshape(group_slots, emb_dim), 0)
    key = jnp.where(valid[:, None], inbox[:, 1].reshape(group_slots, emb_dim), 0)
    first = jnp.sum((bin_owner < dp_index()).astype(jnp.int32))
    allowed = allowed_mask(valid, first, bin_link, group_slots, per_bin)
    grads = contrast(query, key, allowed, valid.astype(jnp.float32))
    back = jnp.stack([g.reshape(sources, per_owner, emb_dim) for g in grads], axis=1)
    returned = lax.all_to_all(
        back.reshape(sources, block, emb_dim), DP, split_axis=0, concat_axis=0, tiled=True
    )
    row_grads = lax.dot_general(
        picks,
        returned.reshape(lanes, emb_dim),
        (((0,), (0,)), ((), ())),
        preferred_element_type=jnp.float32,
    ).reshape(rows_dev, views, emb_dim)
    grad_rows = (
        scale * (row_grads - unit * jnp.sum(unit * row_grads, axis=2, keepdims=True))
    ).astype(jnp.bfloat16)
    column_start = lax.axis_index("bin") * part_rows
    trunk = lax.all_gather(features, "bin", axis=0, tiled=True)
    outgrad = lax.all_to_all(
        jnp.broadcast_to(grad_rows[None], (bins_n, *grad_rows.shape)),
        "bin",
        split_axis=0,
        concat_axis=0,
        tiled=True,
    )
    columns = lax.dynamic_slice_in_dim(trunk, column_start, part_rows, 2)
    count = trunk.shape[0]
    local_grad = lax.dot_general(
        columns.reshape(count * views, part_rows),
        outgrad.reshape(count * views, emb_dim),
        (((0,), (0,)), ((), ())),
        preferred_element_type=jnp.float32,
    )
    sizes = [size for _, size in DP_PARTS]
    per_dev = part_rows // sources
    local_grad = jnp.transpose(local_grad.reshape(*sizes, per_dev, emb_dim), (2, 0, 1, 3, 4))
    kept = lax.dynamic_index_in_dim(local_grad, core, 0, keepdims=False)
    given = lax.dynamic_index_in_dim(local_grad, 1 - core, 0, keepdims=False)
    local_grad = kept + lax.ppermute(given, "dc", perm=[(0, 1), (1, 0)])
    planes = local_grad.reshape(sizes[0] * sizes[1], per_dev, emb_dim).astype(jnp.bfloat16)
    planes = lax.all_to_all(planes, ("dx", "dz"), split_axis=0, concat_axis=0, tiled=True)
    local_grad = jnp.sum(planes.astype(jnp.float32), axis=0)
    grad_weight = local_grad / rows_dev
    return (grad_rows, grad_weight)


def solution(mesh):
    sizes = [size for _, size in DP_PARTS]
    devices = mesh.devices.reshape(*sizes, mesh.devices.shape[1])
    parted = Mesh(devices, (*DP, "bin"))
    return jax.shard_map(
        local,
        mesh=parted,
        in_specs=(P((*DP, "bin"), None, None), P("bin", None), P((*DP, "bin"), None), P(), P()),
        out_specs=(P((*DP, "bin"), None, None), P(("bin", *DP), None)),
        check_vma=False,
    )
```

```python
import jax
import jax.numpy as jnp
from jax import lax
from jax.sharding import Mesh
from jax.sharding import PartitionSpec as P

MOSTB = 2


SOFTMAX_TEMP_SCALE = 0.1

DP_PARTS = (("dx", 4), ("dz", 16), ("dc", 2))
DP = tuple(name for name, _ in DP_PARTS)
EMPTY_MARK = 4.0


def allowed_mask(valid, first, bin_link, group_slots, per_bin):
    per_owner = per_bin * MOSTB
    position = jnp.arange(group_slots, dtype=jnp.int32)
    local_bin = position % per_owner // per_bin
    padded = jnp.concatenate([bin_link, jnp.zeros((MOSTB,), jnp.int32)])
    nearby = lax.dynamic_slice(padded, (first,), (MOSTB,))
    lower = jnp.minimum(local_bin[:, None], local_bin[None, :])
    linked = jnp.zeros((group_slots, group_slots), jnp.int32)
    for height in range(MOSTB):
        linked = linked + jnp.where(lower == height, nearby[height], 0)
    spacing = jnp.abs(local_bin[:, None] - local_bin[None, :])
    paired = valid[:, None] & valid[None, :]
    allowed = paired & ((spacing == 0) | (spacing == 1) & (linked == 1))
    allowed = allowed | (position[:, None] == position[None, :])
    return allowed.astype(jnp.float32)


def contrast(query_rows, key_matrix, allowed, valid):
    similarity_scores = (
        lax.dot_general(
            query_rows, key_matrix, (((1,), (1,)), ((), ())), preferred_element_type=jnp.float32
        )
        / SOFTMAX_TEMP_SCALE
    )
    weights = allowed * jnp.exp(similarity_scores)
    shares = weights / jnp.sum(weights, axis=1, keepdims=True)
    position = jnp.arange(query_rows.shape[0], dtype=jnp.int32)
    diagonal = (position[:, None] == position[None, :]).astype(jnp.float32)
    logit_gradient = ((shares - diagonal) * valid[:, None]).astype(jnp.bfloat16)
    query_gradient = (
        jnp.dot(logit_gradient, key_matrix, preferred_element_type=jnp.float32) / SOFTMAX_TEMP_SCALE
    ).astype(jnp.bfloat16)
    key_gradient_rows = (
        lax.dot_general(
            logit_gradient, query_rows, (((0,), (0,)), ((), ())), preferred_element_type=jnp.float32
        )
        / SOFTMAX_TEMP_SCALE
    ).astype(jnp.bfloat16)
    return query_gradient, key_gradient_rows


def dp_index():
    index = 0
    for name, size in DP_PARTS:
        index = index * size + lax.axis_index(name)
    return index


def local(features, head_weight, bin_of_row, bin_owner, bin_link):
    rows_dev, views, feat_dim = features.shape
    part_rows, emb_dim = head_weight.shape
    sources = 1
    for _, size in DP_PARTS:
        sources *= size
    bins_n = lax.axis_size("bin")
    bin_count = bin_owner.shape[0]
    per_bin = max(2, 2 * rows_dev // bin_count)
    per_owner = per_bin * MOSTB
    group_slots = sources * per_owner
    flat = features.reshape(rows_dev * views, feat_dim)
    core = lax.axis_index("dc")
    halves = head_weight.reshape(2, part_rows // 2, emb_dim)
    half = lax.dynamic_index_in_dim(halves, core, 0, keepdims=False)
    copies = jnp.broadcast_to(half[None], (bins_n, part_rows // 2, emb_dim))
    mine = lax.all_to_all(copies, "bin", split_axis=0, concat_axis=0, tiled=True)
    theirs = lax.ppermute(mine, "dc", perm=[(0, 1), (1, 0)])
    low = jnp.where(core == 0, mine, theirs)
    high = jnp.where(core == 0, theirs, mine)
    weight = jnp.stack([low, high], axis=1).reshape(feat_dim, emb_dim)
    folded = jnp.dot(flat, weight, preferred_element_type=jnp.float32)
    embedded = folded.reshape(rows_dev, views, emb_dim)
    scale = lax.rsqrt(jnp.sum(embedded * embedded, axis=2, keepdims=True) + 1e-06)
    unit = embedded * scale
    sent = unit.astype(jnp.bfloat16)
    row_bins = bin_of_row[:, 0]
    lookup = row_bins[:, None] == jnp.arange(bin_count, dtype=jnp.int32)[None, :]
    owner = jnp.sum(jnp.where(lookup, bin_owner[None, :], 0), axis=1)
    first_by_bin = jnp.sum((bin_owner[None, :] < bin_owner[:, None]).astype(jnp.int32), axis=1)
    local_bin = row_bins - jnp.sum(jnp.where(lookup, first_by_bin[None, :], 0), axis=1)
    order = jnp.arange(rows_dev, dtype=jnp.int32)
    earlier = (row_bins[:, None] == row_bins[None, :]) & (order[None, :] < order[:, None])
    seat = jnp.sum(earlier.astype(jnp.int32), axis=1)
    target = owner * per_owner + local_bin * per_bin + seat
    block = views * per_owner
    dest = (
        (target // per_owner)[:, None] * block
        + jnp.arange(views, dtype=jnp.int32)[None, :] * per_owner
        + (target % per_owner)[:, None]
    )
    lanes = sources * block
    picks = (dest.reshape(-1)[None, :] == jnp.arange(lanes, dtype=jnp.int32)[:, None]).astype(jnp.bfloat16)
    picked = jnp.dot(
        picks, sent.reshape(rows_dev * views, emb_dim), preferred_element_type=jnp.float32
    )
    unfilled = 1.0 - jnp.sum(picks.astype(jnp.float32), axis=1)
    lane_view = jnp.arange(lanes, dtype=jnp.int32) % block // per_owner
    marked = unfilled * (lane_view == 0).astype(jnp.float32) * EMPTY_MARK
    first_lane = (jnp.arange(emb_dim, dtype=jnp.int32) == 0).astype(jnp.float32)
    outbox = (picked + marked[:, None] * first_lane[None, :]).astype(jnp.bfloat16)
    inbox = lax.all_to_all(
        outbox.reshape(sources, block, emb_dim), DP, split_axis=0, concat_axis=0, tiled=True
    )
    inbox = inbox.reshape(sources, views, per_owner, emb_dim)
    valid = (inbox[:, 0, :, 0] < 2.0).reshape(group_slots)
    query = inbox[:, 0].reshape(group_slots, emb_dim)
    key = inbox[:, 1].reshape(group_slots, emb_dim)
    first = jnp.sum((bin_owner < dp_index()).astype(jnp.int32))
    allowed = allowed_mask(valid, first, bin_link, group_slots, per_bin)
    grads = contrast(query, key, allowed, valid.astype(jnp.float32))
    back = jnp.stack([g.reshape(sources, per_owner, emb_dim) for g in grads], axis=1)
    returned = lax.all_to_all(
        back.reshape(sources, block, emb_dim), DP, split_axis=0, concat_axis=0, tiled=True
    )
    row_grads = lax.dot_general(
        picks,
        returned.reshape(lanes, emb_dim),
        (((0,), (0,)), ((), ())),
        preferred_element_type=jnp.float32,
    ).reshape(rows_dev, views, emb_dim)
    grad_rows = (
        scale * (row_grads - unit * jnp.sum(unit * row_grads, axis=2, keepdims=True))
    ).astype(jnp.bfloat16)
    column_start = lax.axis_index("bin") * part_rows
    trunk = lax.all_gather(features, "bin", axis=0, tiled=True)
    outgrad = lax.all_to_all(
        jnp.broadcast_to(grad_rows[None], (bins_n, *grad_rows.shape)),
        "bin",
        split_axis=0,
        concat_axis=0,
        tiled=True,
    )
    columns = lax.dynamic_slice_in_dim(trunk, column_start, part_rows, 2)
    count = trunk.shape[0]
    local_grad = lax.dot_general(
        columns.reshape(count * views, part_rows),
        outgrad.reshape(count * views, emb_dim),
        (((0,), (0,)), ((), ())),
        preferred_element_type=jnp.float32,
    )
    sizes = [size for _, size in DP_PARTS]
    per_dev = part_rows // sources
    local_grad = jnp.transpose(local_grad.reshape(*sizes, per_dev, emb_dim), (2, 0, 1, 3, 4))
    kept = lax.dynamic_index_in_dim(local_grad, core, 0, keepdims=False)
    given = lax.dynamic_index_in_dim(local_grad, 1 - core, 0, keepdims=False)
    local_grad = kept + lax.ppermute(given, "dc", perm=[(0, 1), (1, 0)])
    planes = local_grad.reshape(sizes[0], sizes[1] * per_dev, emb_dim)
    planes = lax.all_to_all(planes, "dx", split_axis=0, concat_axis=0, tiled=True)
    planes = jnp.sum(planes, axis=0).reshape(sizes[1], per_dev, emb_dim).astype(jnp.bfloat16)
    planes = lax.all_to_all(planes, "dz", split_axis=0, concat_axis=0, tiled=True)
    local_grad = jnp.sum(planes.astype(jnp.float32), axis=0)
    grad_weight = local_grad / rows_dev
    return (grad_rows, grad_weight)


def solution(mesh):
    sizes = [size for _, size in DP_PARTS]
    devices = mesh.devices.reshape(*sizes, mesh.devices.shape[1])
    parted = Mesh(devices, (*DP, "bin"))
    return jax.shard_map(
        local,
        mesh=parted,
        in_specs=(P((*DP, "bin"), None, None), P("bin", None), P((*DP, "bin"), None), P(), P()),
        out_specs=(P((*DP, "bin"), None, None), P(("bin", *DP), None)),
        check_vma=False,
    )
```

```python
import jax
import jax.numpy as jnp
from jax import lax
from jax.sharding import Mesh
from jax.sharding import PartitionSpec as P

MOSTB = 2


SOFTMAX_TEMP_SCALE = 0.1

DP_PARTS = (("dx", 4), ("dz", 16), ("dc", 2))
DP = tuple(name for name, _ in DP_PARTS)
EMPTY_MARK = 4.0


def allowed_mask(valid, first, bin_link, group_slots, per_bin):
    per_owner = per_bin * MOSTB
    position = jnp.arange(group_slots, dtype=jnp.int32)
    local_bin = position % per_owner // per_bin
    padded = jnp.concatenate([bin_link, jnp.zeros((MOSTB,), jnp.int32)])
    nearby = lax.dynamic_slice(padded, (first,), (MOSTB,))
    lower = jnp.minimum(local_bin[:, None], local_bin[None, :])
    linked = jnp.zeros((group_slots, group_slots), jnp.int32)
    for height in range(MOSTB):
        linked = linked + jnp.where(lower == height, nearby[height], 0)
    spacing = jnp.abs(local_bin[:, None] - local_bin[None, :])
    paired = valid[:, None] & valid[None, :]
    allowed = paired & ((spacing == 0) | (spacing == 1) & (linked == 1))
    allowed = allowed | (position[:, None] == position[None, :])
    return allowed.astype(jnp.float32)


def contrast(query_rows, key_matrix, allowed, valid):
    similarity_scores = (
        lax.dot_general(
            query_rows, key_matrix, (((1,), (1,)), ((), ())), preferred_element_type=jnp.float32
        )
        / SOFTMAX_TEMP_SCALE
    )
    weights = allowed * jnp.exp(similarity_scores)
    shares = weights / jnp.sum(weights, axis=1, keepdims=True)
    position = jnp.arange(query_rows.shape[0], dtype=jnp.int32)
    diagonal = (position[:, None] == position[None, :]).astype(jnp.float32)
    logit_gradient = ((shares - diagonal) * valid[:, None]).astype(jnp.bfloat16)
    query_gradient = (
        jnp.dot(logit_gradient, key_matrix, preferred_element_type=jnp.float32) / SOFTMAX_TEMP_SCALE
    ).astype(jnp.bfloat16)
    key_gradient_rows = (
        lax.dot_general(
            logit_gradient, query_rows, (((0,), (0,)), ((), ())), preferred_element_type=jnp.float32
        )
        / SOFTMAX_TEMP_SCALE
    ).astype(jnp.bfloat16)
    return query_gradient, key_gradient_rows


def dp_index():
    index = 0
    for name, size in DP_PARTS:
        index = index * size + lax.axis_index(name)
    return index


def local(features, head_weight, bin_of_row, bin_owner, bin_link):
    rows_dev, views, feat_dim = features.shape
    part_rows, emb_dim = head_weight.shape
    sources = 1
    for _, size in DP_PARTS:
        sources *= size
    bins_n = lax.axis_size("bin")
    bin_count = bin_owner.shape[0]
    per_bin = max(2, 2 * rows_dev // bin_count)
    per_owner = per_bin * MOSTB
    group_slots = sources * per_owner
    flat = features.reshape(rows_dev * views, feat_dim)
    core = lax.axis_index("dc")
    halves = head_weight.reshape(2, part_rows // 2, emb_dim)
    half = lax.dynamic_index_in_dim(halves, core, 0, keepdims=False)
    copies = jnp.broadcast_to(half[None], (bins_n, part_rows // 2, emb_dim))
    mine = lax.all_to_all(copies, "bin", split_axis=0, concat_axis=0, tiled=True)
    theirs = lax.ppermute(mine, "dc", perm=[(0, 1), (1, 0)])
    low = jnp.where(core == 0, mine, theirs)
    high = jnp.where(core == 0, theirs, mine)
    weight = jnp.stack([low, high], axis=1).reshape(feat_dim, emb_dim)
    folded = jnp.dot(flat, weight, preferred_element_type=jnp.float32)
    embedded = folded.reshape(rows_dev, views, emb_dim)
    scale = lax.rsqrt(jnp.sum(embedded * embedded, axis=2, keepdims=True) + 1e-06)
    unit = embedded * scale
    sent = unit.astype(jnp.bfloat16)
    row_bins = bin_of_row[:, 0]
    lookup = row_bins[:, None] == jnp.arange(bin_count, dtype=jnp.int32)[None, :]
    owner = jnp.sum(jnp.where(lookup, bin_owner[None, :], 0), axis=1)
    first_by_bin = jnp.sum((bin_owner[None, :] < bin_owner[:, None]).astype(jnp.int32), axis=1)
    local_bin = row_bins - jnp.sum(jnp.where(lookup, first_by_bin[None, :], 0), axis=1)
    order = jnp.arange(rows_dev, dtype=jnp.int32)
    earlier = (row_bins[:, None] == row_bins[None, :]) & (order[None, :] < order[:, None])
    seat = jnp.sum(earlier.astype(jnp.int32), axis=1)
    target = owner * per_owner + local_bin * per_bin + seat
    block = views * per_owner
    dest = (
        (target // per_owner)[:, None] * block
        + jnp.arange(views, dtype=jnp.int32)[None, :] * per_owner
        + (target % per_owner)[:, None]
    )
    lanes = sources * block
    picks = (dest.reshape(-1)[None, :] == jnp.arange(lanes, dtype=jnp.int32)[:, None]).astype(jnp.bfloat16)
    picked = jnp.dot(
        picks, sent.reshape(rows_dev * views, emb_dim), preferred_element_type=jnp.float32
    )
    unfilled = 1.0 - jnp.sum(picks.astype(jnp.float32), axis=1)
    lane_view = jnp.arange(lanes, dtype=jnp.int32) % block // per_owner
    marked = unfilled * (lane_view == 0).astype(jnp.float32) * EMPTY_MARK
    first_lane = (jnp.arange(emb_dim, dtype=jnp.int32) == 0).astype(jnp.float32)
    outbox = (picked + marked[:, None] * first_lane[None, :]).astype(jnp.bfloat16)
    inbox = lax.all_to_all(
        outbox.reshape(sources, block, emb_dim), DP, split_axis=0, concat_axis=0, tiled=True
    )
    inbox = inbox.reshape(sources, views, per_owner, emb_dim)
    valid = (inbox[:, 0, :, 0] < 2.0).reshape(group_slots)
    query = inbox[:, 0].reshape(group_slots, emb_dim)
    key = inbox[:, 1].reshape(group_slots, emb_dim)
    first = jnp.sum((bin_owner < dp_index()).astype(jnp.int32))
    allowed = allowed_mask(valid, first, bin_link, group_slots, per_bin)
    grads = contrast(query, key, allowed, valid.astype(jnp.float32))
    back = jnp.stack([g.reshape(sources, per_owner, emb_dim) for g in grads], axis=1)
    returned = lax.all_to_all(
        back.reshape(sources, block, emb_dim), DP, split_axis=0, concat_axis=0, tiled=True
    )
    row_grads = lax.dot_general(
        picks,
        returned.reshape(lanes, emb_dim),
        (((0,), (0,)), ((), ())),
        preferred_element_type=jnp.float32,
    ).reshape(rows_dev, views, emb_dim)
    grad_rows = (
        scale * (row_grads - unit * jnp.sum(unit * row_grads, axis=2, keepdims=True))
    ).astype(jnp.bfloat16)
    column_start = lax.axis_index("bin") * part_rows
    trunk = lax.all_gather(features, "bin", axis=0, tiled=True)
    outgrad = lax.all_to_all(
        jnp.broadcast_to(grad_rows[None], (bins_n, *grad_rows.shape)),
        "bin",
        split_axis=0,
        concat_axis=0,
        tiled=True,
    )
    columns = lax.dynamic_slice_in_dim(trunk, column_start, part_rows, 2)
    count = trunk.shape[0]
    local_grad = lax.dot_general(
        columns.reshape(count * views, part_rows),
        outgrad.reshape(count * views, emb_dim),
        (((0,), (0,)), ((), ())),
        preferred_element_type=jnp.float32,
    )
    sizes = [size for _, size in DP_PARTS]
    per_dev = part_rows // sources
    local_grad = jnp.transpose(local_grad.reshape(*sizes, per_dev, emb_dim), (2, 0, 1, 3, 4))
    kept = lax.dynamic_index_in_dim(local_grad, core, 0, keepdims=False)
    given = lax.dynamic_index_in_dim(local_grad, 1 - core, 0, keepdims=False)
    local_grad = kept + lax.ppermute(given, "dc", perm=[(0, 1), (1, 0)])
    planes = local_grad.reshape(sizes[0], sizes[1] * per_dev, emb_dim).astype(jnp.bfloat16)
    planes = lax.all_to_all(planes, "dx", split_axis=0, concat_axis=0, tiled=True)
    planes = jnp.sum(planes.astype(jnp.float32), axis=0)
    planes = planes.reshape(sizes[1], per_dev, emb_dim).astype(jnp.bfloat16)
    planes = lax.all_to_all(planes, "dz", split_axis=0, concat_axis=0, tiled=True)
    local_grad = jnp.sum(planes.astype(jnp.float32), axis=0)
    grad_weight = local_grad / rows_dev
    return (grad_rows, grad_weight)


def solution(mesh):
    sizes = [size for _, size in DP_PARTS]
    devices = mesh.devices.reshape(*sizes, mesh.devices.shape[1])
    parted = Mesh(devices, (*DP, "bin"))
    return jax.shard_map(
        local,
        mesh=parted,
        in_specs=(P((*DP, "bin"), None, None), P("bin", None), P((*DP, "bin"), None), P(), P()),
        out_specs=(P((*DP, "bin"), None, None), P(("bin", *DP), None)),
        check_vma=False,
    )
```

```python
import jax
import jax.numpy as jnp
from jax import lax
from jax.sharding import Mesh
from jax.sharding import PartitionSpec as P

MOSTB = 2


SOFTMAX_TEMP_SCALE = 0.1

DP_PARTS = (("dx", 4), ("dzh", 4), ("dzl", 4), ("dc", 2))
DP = tuple(name for name, _ in DP_PARTS)
EMPTY_MARK = 4.0


def allowed_mask(valid, first, bin_link, group_slots, per_bin):
    per_owner = per_bin * MOSTB
    position = jnp.arange(group_slots, dtype=jnp.int32)
    local_bin = position % per_owner // per_bin
    padded = jnp.concatenate([bin_link, jnp.zeros((MOSTB,), jnp.int32)])
    nearby = lax.dynamic_slice(padded, (first,), (MOSTB,))
    lower = jnp.minimum(local_bin[:, None], local_bin[None, :])
    linked = jnp.zeros((group_slots, group_slots), jnp.int32)
    for height in range(MOSTB):
        linked = linked + jnp.where(lower == height, nearby[height], 0)
    spacing = jnp.abs(local_bin[:, None] - local_bin[None, :])
    paired = valid[:, None] & valid[None, :]
    allowed = paired & ((spacing == 0) | (spacing == 1) & (linked == 1))
    allowed = allowed | (position[:, None] == position[None, :])
    return allowed.astype(jnp.float32)


def contrast(query_rows, key_matrix, allowed, valid):
    similarity_scores = (
        lax.dot_general(
            query_rows, key_matrix, (((1,), (1,)), ((), ())), preferred_element_type=jnp.float32
        )
        / SOFTMAX_TEMP_SCALE
    )
    weights = allowed * jnp.exp(similarity_scores)
    shares = weights / jnp.sum(weights, axis=1, keepdims=True)
    position = jnp.arange(query_rows.shape[0], dtype=jnp.int32)
    diagonal = (position[:, None] == position[None, :]).astype(jnp.float32)
    logit_gradient = ((shares - diagonal) * valid[:, None]).astype(jnp.bfloat16)
    query_gradient = (
        jnp.dot(logit_gradient, key_matrix, preferred_element_type=jnp.float32) / SOFTMAX_TEMP_SCALE
    ).astype(jnp.bfloat16)
    key_gradient_rows = (
        lax.dot_general(
            logit_gradient, query_rows, (((0,), (0,)), ((), ())), preferred_element_type=jnp.float32
        )
        / SOFTMAX_TEMP_SCALE
    ).astype(jnp.bfloat16)
    return query_gradient, key_gradient_rows


def dp_index():
    index = 0
    for name, size in DP_PARTS:
        index = index * size + lax.axis_index(name)
    return index


def local(features, head_weight, bin_of_row, bin_owner, bin_link):
    rows_dev, views, feat_dim = features.shape
    part_rows, emb_dim = head_weight.shape
    sources = 1
    for _, size in DP_PARTS:
        sources *= size
    bins_n = lax.axis_size("bin")
    bin_count = bin_owner.shape[0]
    per_bin = max(2, 2 * rows_dev // bin_count)
    per_owner = per_bin * MOSTB
    group_slots = sources * per_owner
    flat = features.reshape(rows_dev * views, feat_dim)
    core = lax.axis_index("dc")
    halves = head_weight.reshape(2, part_rows // 2, emb_dim)
    half = lax.dynamic_index_in_dim(halves, core, 0, keepdims=False)
    copies = jnp.broadcast_to(half[None], (bins_n, part_rows // 2, emb_dim))
    mine = lax.all_to_all(copies, "bin", split_axis=0, concat_axis=0, tiled=True)
    theirs = lax.ppermute(mine, "dc", perm=[(0, 1), (1, 0)])
    low = jnp.where(core == 0, mine, theirs)
    high = jnp.where(core == 0, theirs, mine)
    weight = jnp.stack([low, high], axis=1).reshape(feat_dim, emb_dim)
    folded = jnp.dot(flat, weight, preferred_element_type=jnp.float32)
    embedded = folded.reshape(rows_dev, views, emb_dim)
    scale = lax.rsqrt(jnp.sum(embedded * embedded, axis=2, keepdims=True) + 1e-06)
    unit = embedded * scale
    sent = unit.astype(jnp.bfloat16)
    row_bins = bin_of_row[:, 0]
    lookup = row_bins[:, None] == jnp.arange(bin_count, dtype=jnp.int32)[None, :]
    owner = jnp.sum(jnp.where(lookup, bin_owner[None, :], 0), axis=1)
    first_by_bin = jnp.sum((bin_owner[None, :] < bin_owner[:, None]).astype(jnp.int32), axis=1)
    local_bin = row_bins - jnp.sum(jnp.where(lookup, first_by_bin[None, :], 0), axis=1)
    order = jnp.arange(rows_dev, dtype=jnp.int32)
    earlier = (row_bins[:, None] == row_bins[None, :]) & (order[None, :] < order[:, None])
    seat = jnp.sum(earlier.astype(jnp.int32), axis=1)
    target = owner * per_owner + local_bin * per_bin + seat
    block = views * per_owner
    dest = (
        (target // per_owner)[:, None] * block
        + jnp.arange(views, dtype=jnp.int32)[None, :] * per_owner
        + (target % per_owner)[:, None]
    )
    lanes = sources * block
    picks = (dest.reshape(-1)[None, :] == jnp.arange(lanes, dtype=jnp.int32)[:, None]).astype(jnp.bfloat16)
    picked = jnp.dot(
        picks, sent.reshape(rows_dev * views, emb_dim), preferred_element_type=jnp.float32
    )
    unfilled = 1.0 - jnp.sum(picks.astype(jnp.float32), axis=1)
    lane_view = jnp.arange(lanes, dtype=jnp.int32) % block // per_owner
    marked = unfilled * (lane_view == 0).astype(jnp.float32) * EMPTY_MARK
    first_lane = (jnp.arange(emb_dim, dtype=jnp.int32) == 0).astype(jnp.float32)
    outbox = (picked + marked[:, None] * first_lane[None, :]).astype(jnp.bfloat16)
    inbox = lax.all_to_all(
        outbox.reshape(sources, block, emb_dim), DP, split_axis=0, concat_axis=0, tiled=True
    )
    inbox = inbox.reshape(sources, views, per_owner, emb_dim)
    valid = (inbox[:, 0, :, 0] < 2.0).reshape(group_slots)
    query = inbox[:, 0].reshape(group_slots, emb_dim)
    key = inbox[:, 1].reshape(group_slots, emb_dim)
    first = jnp.sum((bin_owner < dp_index()).astype(jnp.int32))
    allowed = allowed_mask(valid, first, bin_link, group_slots, per_bin)
    grads = contrast(query, key, allowed, valid.astype(jnp.float32))
    back = jnp.stack([g.reshape(sources, per_owner, emb_dim) for g in grads], axis=1)
    returned = lax.all_to_all(
        back.reshape(sources, block, emb_dim), DP, split_axis=0, concat_axis=0, tiled=True
    )
    row_grads = lax.dot_general(
        picks,
        returned.reshape(lanes, emb_dim),
        (((0,), (0,)), ((), ())),
        preferred_element_type=jnp.float32,
    ).reshape(rows_dev, views, emb_dim)
    grad_rows = (
        scale * (row_grads - unit * jnp.sum(unit * row_grads, axis=2, keepdims=True))
    ).astype(jnp.bfloat16)
    column_start = lax.axis_index("bin") * part_rows
    trunk = lax.all_gather(features, "bin", axis=0, tiled=True)
    outgrad = lax.all_to_all(
        jnp.broadcast_to(grad_rows[None], (bins_n, *grad_rows.shape)),
        "bin",
        split_axis=0,
        concat_axis=0,
        tiled=True,
    )
    columns = lax.dynamic_slice_in_dim(trunk, column_start, part_rows, 2)
    count = trunk.shape[0]
    local_grad = lax.dot_general(
        columns.reshape(count * views, part_rows),
        outgrad.reshape(count * views, emb_dim),
        (((0,), (0,)), ((), ())),
        preferred_element_type=jnp.float32,
    )
    sizes = [size for _, size in DP_PARTS]
    per_dev = part_rows // sources
    local_grad = jnp.transpose(local_grad.reshape(*sizes, per_dev, emb_dim), (3, 0, 1, 2, 4, 5))
    kept = lax.dynamic_index_in_dim(local_grad, core, 0, keepdims=False)
    given = lax.dynamic_index_in_dim(local_grad, 1 - core, 0, keepdims=False)
    local_grad = kept + lax.ppermute(given, "dc", perm=[(0, 1), (1, 0)])
    planes = local_grad.reshape(sizes[0], -1, emb_dim).astype(jnp.bfloat16)
    planes = lax.all_to_all(planes, "dx", split_axis=0, concat_axis=0, tiled=True)
    planes = jnp.sum(planes.astype(jnp.float32), axis=0).reshape(sizes[1], sizes[2], per_dev, emb_dim)
    planes = jnp.transpose(planes, (1, 0, 2, 3)).reshape(sizes[2], -1, emb_dim).astype(jnp.bfloat16)
    planes = lax.all_to_all(planes, "dzl", split_axis=0, concat_axis=0, tiled=True)
    planes = jnp.sum(planes.astype(jnp.float32), axis=0).reshape(sizes[1], per_dev, emb_dim)
    planes = lax.all_to_all(planes, "dzh", split_axis=0, concat_axis=0, tiled=True)
    local_grad = jnp.sum(planes, axis=0)
    grad_weight = local_grad / rows_dev
    return (grad_rows, grad_weight)


def solution(mesh):
    sizes = [size for _, size in DP_PARTS]
    devices = mesh.devices.reshape(*sizes, mesh.devices.shape[1])
    parted = Mesh(devices, (*DP, "bin"))
    return jax.shard_map(
        local,
        mesh=parted,
        in_specs=(P((*DP, "bin"), None, None), P("bin", None), P((*DP, "bin"), None), P(), P()),
        out_specs=(P((*DP, "bin"), None, None), P(("bin", *DP), None)),
        check_vma=False,
    )
```

```python
import jax
import jax.numpy as jnp
from jax import lax
from jax.sharding import Mesh
from jax.sharding import PartitionSpec as P

MOSTB = 2


SOFTMAX_TEMP_SCALE = 0.1

DP_PARTS = (("dx", 4), ("dz", 16), ("dc", 2))
DP = tuple(name for name, _ in DP_PARTS)
EMPTY_MARK = 4.0


def allowed_mask(valid, first, bin_link, group_slots, per_bin):
    per_owner = per_bin * MOSTB
    position = jnp.arange(group_slots, dtype=jnp.int32)
    local_bin = position % per_owner // per_bin
    padded = jnp.concatenate([bin_link, jnp.zeros((MOSTB,), jnp.int32)])
    nearby = lax.dynamic_slice(padded, (first,), (MOSTB,))
    lower = jnp.minimum(local_bin[:, None], local_bin[None, :])
    linked = jnp.zeros((group_slots, group_slots), jnp.int32)
    for height in range(MOSTB):
        linked = linked + jnp.where(lower == height, nearby[height], 0)
    spacing = jnp.abs(local_bin[:, None] - local_bin[None, :])
    paired = valid[:, None] & valid[None, :]
    allowed = paired & ((spacing == 0) | (spacing == 1) & (linked == 1))
    allowed = allowed | (position[:, None] == position[None, :])
    return allowed.astype(jnp.float32)


def contrast(query_rows, key_matrix, allowed, valid):
    similarity_scores = (
        lax.dot_general(
            query_rows, key_matrix, (((1,), (1,)), ((), ())), preferred_element_type=jnp.float32
        )
        / SOFTMAX_TEMP_SCALE
    )
    weights = allowed * jnp.exp(similarity_scores)
    shares = weights / jnp.sum(weights, axis=1, keepdims=True)
    position = jnp.arange(query_rows.shape[0], dtype=jnp.int32)
    diagonal = (position[:, None] == position[None, :]).astype(jnp.float32)
    logit_gradient = ((shares - diagonal) * valid[:, None]).astype(jnp.bfloat16)
    query_gradient = (
        jnp.dot(logit_gradient, key_matrix, preferred_element_type=jnp.float32) / SOFTMAX_TEMP_SCALE
    ).astype(jnp.bfloat16)
    key_gradient_rows = (
        lax.dot_general(
            logit_gradient, query_rows, (((0,), (0,)), ((), ())), preferred_element_type=jnp.float32
        )
        / SOFTMAX_TEMP_SCALE
    ).astype(jnp.bfloat16)
    return query_gradient, key_gradient_rows


def dp_index():
    index = 0
    for name, size in DP_PARTS:
        index = index * size + lax.axis_index(name)
    return index


def local(features, head_weight, bin_of_row, bin_owner, bin_link):
    rows_dev, views, feat_dim = features.shape
    part_rows, emb_dim = head_weight.shape
    sources = 1
    for _, size in DP_PARTS:
        sources *= size
    bins_n = lax.axis_size("bin")
    bin_count = bin_owner.shape[0]
    per_bin = max(2, 2 * rows_dev // bin_count)
    per_owner = per_bin * MOSTB
    group_slots = sources * per_owner
    flat = features.reshape(rows_dev * views, feat_dim)
    core = lax.axis_index("dc")
    halves = head_weight.reshape(2, part_rows // 2, emb_dim)
    half = lax.dynamic_index_in_dim(halves, core, 0, keepdims=False)
    copies = jnp.broadcast_to(half[None], (bins_n, part_rows // 2, emb_dim))
    mine = lax.all_to_all(copies, "bin", split_axis=0, concat_axis=0, tiled=True)
    theirs = lax.ppermute(mine, "dc", perm=[(0, 1), (1, 0)])
    low = jnp.where(core == 0, mine, theirs)
    high = jnp.where(core == 0, theirs, mine)
    weight = jnp.stack([low, high], axis=1).reshape(feat_dim, emb_dim)
    folded = jnp.dot(flat, weight, preferred_element_type=jnp.float32)
    scale = lax.rsqrt(jnp.sum(folded * folded, axis=1, keepdims=True) + 1e-06)
    unit = folded * scale
    sent = unit.astype(jnp.bfloat16)
    row_bins = bin_of_row[:, 0]
    lookup = row_bins[:, None] == jnp.arange(bin_count, dtype=jnp.int32)[None, :]
    owner = jnp.sum(jnp.where(lookup, bin_owner[None, :], 0), axis=1)
    first_by_bin = jnp.sum((bin_owner[None, :] < bin_owner[:, None]).astype(jnp.int32), axis=1)
    local_bin = row_bins - jnp.sum(jnp.where(lookup, first_by_bin[None, :], 0), axis=1)
    order = jnp.arange(rows_dev, dtype=jnp.int32)
    earlier = (row_bins[:, None] == row_bins[None, :]) & (order[None, :] < order[:, None])
    seat = jnp.sum(earlier.astype(jnp.int32), axis=1)
    target = owner * per_owner + local_bin * per_bin + seat
    block = views * per_owner
    dest = (
        (target // per_owner)[:, None] * block
        + jnp.arange(views, dtype=jnp.int32)[None, :] * per_owner
        + (target % per_owner)[:, None]
    )
    lanes = sources * block
    picks = (dest.reshape(-1)[None, :] == jnp.arange(lanes, dtype=jnp.int32)[:, None]).astype(jnp.bfloat16)
    picked = jnp.dot(
        picks, sent, preferred_element_type=jnp.float32
    )
    unfilled = 1.0 - jnp.sum(picks.astype(jnp.float32), axis=1)
    lane_view = jnp.arange(lanes, dtype=jnp.int32) % block // per_owner
    marked = unfilled * (lane_view == 0).astype(jnp.float32) * EMPTY_MARK
    first_lane = (jnp.arange(emb_dim, dtype=jnp.int32) == 0).astype(jnp.float32)
    outbox = (picked + marked[:, None] * first_lane[None, :]).astype(jnp.bfloat16)
    inbox = lax.all_to_all(
        outbox.reshape(sources, block, emb_dim), DP, split_axis=0, concat_axis=0, tiled=True
    )
    inbox = inbox.reshape(sources, views, per_owner, emb_dim)
    valid = (inbox[:, 0, :, 0] < 2.0).reshape(group_slots)
    query = inbox[:, 0].reshape(group_slots, emb_dim)
    key = inbox[:, 1].reshape(group_slots, emb_dim)
    first = jnp.sum((bin_owner < dp_index()).astype(jnp.int32))
    allowed = allowed_mask(valid, first, bin_link, group_slots, per_bin)
    grads = contrast(query, key, allowed, valid.astype(jnp.float32))
    back = jnp.stack([g.reshape(sources, per_owner, emb_dim) for g in grads], axis=1)
    returned = lax.all_to_all(
        back.reshape(sources, block, emb_dim), DP, split_axis=0, concat_axis=0, tiled=True
    )
    row_grads = lax.dot_general(
        picks,
        returned.reshape(lanes, emb_dim),
        (((0,), (0,)), ((), ())),
        preferred_element_type=jnp.float32,
    )
    flat_grads = (
        scale * (row_grads - unit * jnp.sum(unit * row_grads, axis=1, keepdims=True))
    ).astype(jnp.bfloat16)
    grad_rows = flat_grads.reshape(rows_dev, views, emb_dim)
    column_start = lax.axis_index("bin") * part_rows
    trunk = lax.all_gather(flat, "bin", axis=0, tiled=True)
    outgrad = lax.all_to_all(
        jnp.broadcast_to(flat_grads[None], (bins_n, *flat_grads.shape)),
        "bin",
        split_axis=0,
        concat_axis=0,
        tiled=True,
    )
    columns = lax.dynamic_slice_in_dim(trunk, column_start, part_rows, 1)
    local_grad = lax.dot_general(
        columns,
        outgrad.reshape(-1, emb_dim),
        (((0,), (0,)), ((), ())),
        preferred_element_type=jnp.float32,
    )
    sizes = [size for _, size in DP_PARTS]
    per_dev = part_rows // sources
    local_grad = jnp.transpose(local_grad.reshape(*sizes, per_dev, emb_dim), (2, 0, 1, 3, 4))
    kept = lax.dynamic_index_in_dim(local_grad, core, 0, keepdims=False)
    given = lax.dynamic_index_in_dim(local_grad, 1 - core, 0, keepdims=False)
    local_grad = kept + lax.ppermute(given, "dc", perm=[(0, 1), (1, 0)])
    planes = local_grad.reshape(sizes[0], sizes[1] * per_dev, emb_dim).astype(jnp.bfloat16)
    planes = lax.all_to_all(planes, "dx", split_axis=0, concat_axis=0, tiled=True)
    planes = jnp.sum(planes.astype(jnp.float32), axis=0)
    planes = planes.reshape(sizes[1], per_dev, emb_dim).astype(jnp.bfloat16)
    planes = lax.all_to_all(planes, "dz", split_axis=0, concat_axis=0, tiled=True)
    local_grad = jnp.sum(planes.astype(jnp.float32), axis=0)
    grad_weight = local_grad / rows_dev
    return (grad_rows, grad_weight)


def solution(mesh):
    sizes = [size for _, size in DP_PARTS]
    devices = mesh.devices.reshape(*sizes, mesh.devices.shape[1])
    parted = Mesh(devices, (*DP, "bin"))
    return jax.shard_map(
        local,
        mesh=parted,
        in_specs=(P((*DP, "bin"), None, None), P("bin", None), P((*DP, "bin"), None), P(), P()),
        out_specs=(P((*DP, "bin"), None, None), P(("bin", *DP), None)),
        check_vma=False,
    )
```

```python
import jax
import jax.numpy as jnp
from jax import lax
from jax.sharding import Mesh
from jax.sharding import PartitionSpec as P

MOSTB = 2


SOFTMAX_TEMP_SCALE = 0.1

DP_PARTS = (("dx", 4), ("dz", 16), ("dc", 2))
DP = tuple(name for name, _ in DP_PARTS)
EMPTY_MARK = 4.0


def allowed_mask(valid, first, bin_link, group_slots, per_bin):
    per_owner = per_bin * MOSTB
    position = jnp.arange(group_slots, dtype=jnp.int32)
    local_bin = position % per_owner // per_bin
    padded = jnp.concatenate([bin_link, jnp.zeros((MOSTB,), jnp.int32)])
    nearby = lax.dynamic_slice(padded, (first,), (MOSTB,))
    lower = jnp.minimum(local_bin[:, None], local_bin[None, :])
    linked = jnp.zeros((group_slots, group_slots), jnp.int32)
    for height in range(MOSTB):
        linked = linked + jnp.where(lower == height, nearby[height], 0)
    spacing = jnp.abs(local_bin[:, None] - local_bin[None, :])
    paired = valid[:, None] & valid[None, :]
    allowed = paired & ((spacing == 0) | (spacing == 1) & (linked == 1))
    allowed = allowed | (position[:, None] == position[None, :])
    return allowed.astype(jnp.float32)


def contrast(query_rows, key_matrix, allowed, valid):
    similarity_scores = (
        lax.dot_general(
            query_rows, key_matrix, (((1,), (1,)), ((), ())), preferred_element_type=jnp.float32
        )
        / SOFTMAX_TEMP_SCALE
    )
    weights = allowed * jnp.exp(similarity_scores)
    shares = weights / jnp.sum(weights, axis=1, keepdims=True)
    position = jnp.arange(query_rows.shape[0], dtype=jnp.int32)
    diagonal = (position[:, None] == position[None, :]).astype(jnp.float32)
    logit_gradient = ((shares - diagonal) * valid[:, None]).astype(jnp.bfloat16)
    query_gradient = (
        jnp.dot(logit_gradient, key_matrix, preferred_element_type=jnp.float32) / SOFTMAX_TEMP_SCALE
    ).astype(jnp.bfloat16)
    key_gradient_rows = (
        lax.dot_general(
            logit_gradient, query_rows, (((0,), (0,)), ((), ())), preferred_element_type=jnp.float32
        )
        / SOFTMAX_TEMP_SCALE
    ).astype(jnp.bfloat16)
    return query_gradient, key_gradient_rows


def dp_index():
    index = 0
    for name, size in DP_PARTS:
        index = index * size + lax.axis_index(name)
    return index


def local(features, head_weight, bin_of_row, bin_owner, bin_link):
    rows_dev, views, feat_dim = features.shape
    part_rows, emb_dim = head_weight.shape
    sources = 1
    for _, size in DP_PARTS:
        sources *= size
    bins_n = lax.axis_size("bin")
    bin_count = bin_owner.shape[0]
    per_bin = max(2, 2 * rows_dev // bin_count)
    per_owner = per_bin * MOSTB
    group_slots = sources * per_owner
    flat = features.reshape(rows_dev * views, feat_dim)
    core = lax.axis_index("dc")
    halves = head_weight.reshape(2, part_rows // 2, emb_dim)
    half = lax.dynamic_index_in_dim(halves, core, 0, keepdims=False)
    copies = jnp.broadcast_to(half[None], (bins_n, part_rows // 2, emb_dim))
    mine = lax.all_to_all(copies, "bin", split_axis=0, concat_axis=0, tiled=True)
    theirs = lax.ppermute(mine, "dc", perm=[(0, 1), (1, 0)])
    low = jnp.where(core == 0, mine, theirs)
    high = jnp.where(core == 0, theirs, mine)
    weight = jnp.stack([low, high], axis=1).reshape(feat_dim, emb_dim)
    folded = jnp.dot(flat, weight, preferred_element_type=jnp.float32)
    embedded = folded.reshape(rows_dev, views, emb_dim)
    scale = lax.rsqrt(jnp.sum(embedded * embedded, axis=2, keepdims=True) + 1e-06)
    unit = embedded * scale
    sent = unit.astype(jnp.bfloat16)
    row_bins = bin_of_row[:, 0]
    lookup = row_bins[:, None] == jnp.arange(bin_count, dtype=jnp.int32)[None, :]
    owner = jnp.sum(jnp.where(lookup, bin_owner[None, :], 0), axis=1)
    first_by_bin = jnp.sum((bin_owner[None, :] < bin_owner[:, None]).astype(jnp.int32), axis=1)
    local_bin = row_bins - jnp.sum(jnp.where(lookup, first_by_bin[None, :], 0), axis=1)
    order = jnp.arange(rows_dev, dtype=jnp.int32)
    earlier = (row_bins[:, None] == row_bins[None, :]) & (order[None, :] < order[:, None])
    seat = jnp.sum(earlier.astype(jnp.int32), axis=1)
    target = owner * per_owner + local_bin * per_bin + seat
    block = views * per_owner
    dest = (
        (target // per_owner)[:, None] * block
        + jnp.arange(views, dtype=jnp.int32)[None, :] * per_owner
        + (target % per_owner)[:, None]
    )
    lanes = sources * block
    picks = (dest.reshape(-1)[None, :] == jnp.arange(lanes, dtype=jnp.int32)[:, None]).astype(jnp.bfloat16)
    picked = jnp.dot(
        picks, sent.reshape(rows_dev * views, emb_dim), preferred_element_type=jnp.float32
    )
    unfilled = 1.0 - jnp.sum(picks.astype(jnp.float32), axis=1)
    lane_view = jnp.arange(lanes, dtype=jnp.int32) % block // per_owner
    marked = unfilled * (lane_view == 0).astype(jnp.float32) * EMPTY_MARK
    first_lane = (jnp.arange(emb_dim, dtype=jnp.int32) == 0).astype(jnp.float32)
    outbox = (picked + marked[:, None] * first_lane[None, :]).astype(jnp.bfloat16)
    inbox = lax.all_to_all(
        outbox.reshape(sources, block, emb_dim), DP, split_axis=0, concat_axis=0, tiled=True
    )
    inbox = inbox.reshape(sources, views, per_owner, emb_dim)
    columns = lax.all_to_all(
        flat.reshape(rows_dev * views, bins_n, part_rows), "bin", split_axis=1, concat_axis=0, tiled=True
    ).reshape(bins_n * rows_dev * views, part_rows)
    inbox, columns = lax.optimization_barrier((inbox, columns))
    valid = (inbox[:, 0, :, 0] < 2.0).reshape(group_slots)
    query = inbox[:, 0].reshape(group_slots, emb_dim)
    key = inbox[:, 1].reshape(group_slots, emb_dim)
    first = jnp.sum((bin_owner < dp_index()).astype(jnp.int32))
    allowed = allowed_mask(valid, first, bin_link, group_slots, per_bin)
    grads = contrast(query, key, allowed, valid.astype(jnp.float32))
    back = jnp.stack([g.reshape(sources, per_owner, emb_dim) for g in grads], axis=1)
    returned = lax.all_to_all(
        back.reshape(sources, block, emb_dim), DP, split_axis=0, concat_axis=0, tiled=True
    )
    row_grads = lax.dot_general(
        picks,
        returned.reshape(lanes, emb_dim),
        (((0,), (0,)), ((), ())),
        preferred_element_type=jnp.float32,
    ).reshape(rows_dev, views, emb_dim)
    grad_rows = (
        scale * (row_grads - unit * jnp.sum(unit * row_grads, axis=2, keepdims=True))
    ).astype(jnp.bfloat16)
    outgrad = lax.all_to_all(
        jnp.broadcast_to(grad_rows[None], (bins_n, *grad_rows.shape)),
        "bin",
        split_axis=0,
        concat_axis=0,
        tiled=True,
    )
    local_grad = lax.dot_general(
        columns,
        outgrad.reshape(-1, emb_dim),
        (((0,), (0,)), ((), ())),
        preferred_element_type=jnp.float32,
    )
    sizes = [size for _, size in DP_PARTS]
    per_dev = part_rows // sources
    local_grad = jnp.transpose(local_grad.reshape(*sizes, per_dev, emb_dim), (2, 0, 1, 3, 4))
    kept = lax.dynamic_index_in_dim(local_grad, core, 0, keepdims=False)
    given = lax.dynamic_index_in_dim(local_grad, 1 - core, 0, keepdims=False)
    local_grad = kept + lax.ppermute(given, "dc", perm=[(0, 1), (1, 0)])
    planes = local_grad.reshape(sizes[0], sizes[1] * per_dev, emb_dim).astype(jnp.bfloat16)
    planes = lax.all_to_all(planes, "dx", split_axis=0, concat_axis=0, tiled=True)
    planes = jnp.sum(planes.astype(jnp.float32), axis=0)
    planes = planes.reshape(sizes[1], per_dev, emb_dim).astype(jnp.bfloat16)
    planes = lax.all_to_all(planes, "dz", split_axis=0, concat_axis=0, tiled=True)
    local_grad = jnp.sum(planes.astype(jnp.float32), axis=0)
    grad_weight = local_grad / rows_dev
    return (grad_rows, grad_weight)


def solution(mesh):
    sizes = [size for _, size in DP_PARTS]
    devices = mesh.devices.reshape(*sizes, mesh.devices.shape[1])
    parted = Mesh(devices, (*DP, "bin"))
    return jax.shard_map(
        local,
        mesh=parted,
        in_specs=(P((*DP, "bin"), None, None), P("bin", None), P((*DP, "bin"), None), P(), P()),
        out_specs=(P((*DP, "bin"), None, None), P(("bin", *DP), None)),
        check_vma=False,
    )
```

```python
import jax
import jax.numpy as jnp
from jax import lax
from jax.sharding import Mesh
from jax.sharding import PartitionSpec as P

MOSTB = 2


SOFTMAX_TEMP_SCALE = 0.1

DP_PARTS = (("dx", 4), ("dz", 16), ("dc", 2))
DP = tuple(name for name, _ in DP_PARTS)
EMPTY_MARK = 4.0


def allowed_mask(valid, first, bin_link, group_slots, per_bin):
    per_owner = per_bin * MOSTB
    position = jnp.arange(group_slots, dtype=jnp.int32)
    local_bin = position % per_owner // per_bin
    padded = jnp.concatenate([bin_link, jnp.zeros((MOSTB,), jnp.int32)])
    nearby = lax.dynamic_slice(padded, (first,), (MOSTB,))
    lower = jnp.minimum(local_bin[:, None], local_bin[None, :])
    linked = jnp.zeros((group_slots, group_slots), jnp.int32)
    for height in range(MOSTB):
        linked = linked + jnp.where(lower == height, nearby[height], 0)
    spacing = jnp.abs(local_bin[:, None] - local_bin[None, :])
    paired = valid[:, None] & valid[None, :]
    allowed = paired & ((spacing == 0) | (spacing == 1) & (linked == 1))
    allowed = allowed | (position[:, None] == position[None, :])
    return allowed.astype(jnp.float32)


def contrast(query_rows, key_matrix, allowed, valid):
    similarity_scores = (
        lax.dot_general(
            query_rows, key_matrix, (((1,), (1,)), ((), ())), preferred_element_type=jnp.float32
        )
        / SOFTMAX_TEMP_SCALE
    )
    weights = allowed * jnp.exp(similarity_scores)
    shares = weights / jnp.sum(weights, axis=1, keepdims=True)
    position = jnp.arange(query_rows.shape[0], dtype=jnp.int32)
    diagonal = (position[:, None] == position[None, :]).astype(jnp.float32)
    logit_gradient = ((shares - diagonal) * valid[:, None]).astype(jnp.bfloat16)
    query_gradient = (
        jnp.dot(logit_gradient, key_matrix, preferred_element_type=jnp.float32) / SOFTMAX_TEMP_SCALE
    ).astype(jnp.bfloat16)
    key_gradient_rows = (
        lax.dot_general(
            logit_gradient, query_rows, (((0,), (0,)), ((), ())), preferred_element_type=jnp.float32
        )
        / SOFTMAX_TEMP_SCALE
    ).astype(jnp.bfloat16)
    return query_gradient, key_gradient_rows


def dp_index():
    index = 0
    for name, size in DP_PARTS:
        index = index * size + lax.axis_index(name)
    return index


def local(features, head_weight, bin_of_row, bin_owner, bin_link):
    rows_dev, views, feat_dim = features.shape
    part_rows, emb_dim = head_weight.shape
    sources = 1
    for _, size in DP_PARTS:
        sources *= size
    bins_n = lax.axis_size("bin")
    bin_count = bin_owner.shape[0]
    per_bin = max(2, 2 * rows_dev // bin_count)
    per_owner = per_bin * MOSTB
    group_slots = sources * per_owner
    flat = features.reshape(rows_dev * views, feat_dim)
    core = lax.axis_index("dc")
    halves = head_weight.reshape(2, part_rows // 2, emb_dim)
    half = lax.dynamic_index_in_dim(halves, core, 0, keepdims=False)
    copies = jnp.broadcast_to(half[None], (bins_n, part_rows // 2, emb_dim))
    mine = lax.all_to_all(copies, "bin", split_axis=0, concat_axis=0, tiled=True)
    theirs = lax.ppermute(mine, "dc", perm=[(0, 1), (1, 0)])
    low = jnp.where(core == 0, mine, theirs)
    high = jnp.where(core == 0, theirs, mine)
    weight = jnp.stack([low, high], axis=1).reshape(feat_dim, emb_dim)
    folded = jnp.dot(flat, weight, preferred_element_type=jnp.float32)
    embedded = folded.reshape(rows_dev, views, emb_dim)
    scale = lax.rsqrt(jnp.sum(embedded * embedded, axis=2, keepdims=True) + 1e-06)
    unit = embedded * scale
    sent = unit.astype(jnp.bfloat16)
    row_bins = bin_of_row[:, 0]
    lookup = row_bins[:, None] == jnp.arange(bin_count, dtype=jnp.int32)[None, :]
    owner = jnp.sum(jnp.where(lookup, bin_owner[None, :], 0), axis=1)
    first_by_bin = jnp.sum((bin_owner[None, :] < bin_owner[:, None]).astype(jnp.int32), axis=1)
    local_bin = row_bins - jnp.sum(jnp.where(lookup, first_by_bin[None, :], 0), axis=1)
    order = jnp.arange(rows_dev, dtype=jnp.int32)
    earlier = (row_bins[:, None] == row_bins[None, :]) & (order[None, :] < order[:, None])
    seat = jnp.sum(earlier.astype(jnp.int32), axis=1)
    target = owner * per_owner + local_bin * per_bin + seat
    block = views * per_owner
    dest = (
        (target // per_owner)[:, None] * block
        + jnp.arange(views, dtype=jnp.int32)[None, :] * per_owner
        + (target % per_owner)[:, None]
    )
    lanes = sources * block
    picks = (dest.reshape(-1)[None, :] == jnp.arange(lanes, dtype=jnp.int32)[:, None]).astype(jnp.bfloat16)
    picked = jnp.dot(
        picks, sent.reshape(rows_dev * views, emb_dim), preferred_element_type=jnp.float32
    )
    unfilled = 1.0 - jnp.sum(picks.astype(jnp.float32), axis=1)
    lane_view = jnp.arange(lanes, dtype=jnp.int32) % block // per_owner
    marked = unfilled * (lane_view == 0).astype(jnp.float32) * EMPTY_MARK
    first_lane = (jnp.arange(emb_dim, dtype=jnp.int32) == 0).astype(jnp.float32)
    outbox = (picked + marked[:, None] * first_lane[None, :]).astype(jnp.bfloat16)
    inbox = lax.all_to_all(
        outbox.reshape(sources, block, emb_dim), DP, split_axis=0, concat_axis=0, tiled=True
    )
    inbox = inbox.reshape(sources, views, per_owner, emb_dim)
    columns = lax.all_to_all(
        flat.reshape(rows_dev * views, bins_n, part_rows), "bin", split_axis=1, concat_axis=0, tiled=True
    ).reshape(bins_n * rows_dev * views, part_rows)
    valid = (inbox[:, 0, :, 0] < 2.0).reshape(group_slots)
    query = inbox[:, 0].reshape(group_slots, emb_dim)
    key = inbox[:, 1].reshape(group_slots, emb_dim)
    first = jnp.sum((bin_owner < dp_index()).astype(jnp.int32))
    allowed = allowed_mask(valid, first, bin_link, group_slots, per_bin)
    grads = contrast(query, key, allowed, valid.astype(jnp.float32))
    back = jnp.stack([g.reshape(sources, per_owner, emb_dim) for g in grads], axis=1)
    back, columns = lax.optimization_barrier((back, columns))
    returned = lax.all_to_all(
        back.reshape(sources, block, emb_dim), DP, split_axis=0, concat_axis=0, tiled=True
    )
    row_grads = lax.dot_general(
        picks,
        returned.reshape(lanes, emb_dim),
        (((0,), (0,)), ((), ())),
        preferred_element_type=jnp.float32,
    ).reshape(rows_dev, views, emb_dim)
    grad_rows = (
        scale * (row_grads - unit * jnp.sum(unit * row_grads, axis=2, keepdims=True))
    ).astype(jnp.bfloat16)
    outgrad = lax.all_to_all(
        jnp.broadcast_to(grad_rows[None], (bins_n, *grad_rows.shape)),
        "bin",
        split_axis=0,
        concat_axis=0,
        tiled=True,
    )
    local_grad = lax.dot_general(
        columns,
        outgrad.reshape(-1, emb_dim),
        (((0,), (0,)), ((), ())),
        preferred_element_type=jnp.float32,
    )
    sizes = [size for _, size in DP_PARTS]
    per_dev = part_rows // sources
    local_grad = jnp.transpose(local_grad.reshape(*sizes, per_dev, emb_dim), (2, 0, 1, 3, 4))
    kept = lax.dynamic_index_in_dim(local_grad, core, 0, keepdims=False)
    given = lax.dynamic_index_in_dim(local_grad, 1 - core, 0, keepdims=False)
    local_grad = kept + lax.ppermute(given, "dc", perm=[(0, 1), (1, 0)])
    planes = local_grad.reshape(sizes[0], sizes[1] * per_dev, emb_dim).astype(jnp.bfloat16)
    planes = lax.all_to_all(planes, "dx", split_axis=0, concat_axis=0, tiled=True)
    planes = jnp.sum(planes.astype(jnp.float32), axis=0)
    planes = planes.reshape(sizes[1], per_dev, emb_dim).astype(jnp.bfloat16)
    planes = lax.all_to_all(planes, "dz", split_axis=0, concat_axis=0, tiled=True)
    local_grad = jnp.sum(planes.astype(jnp.float32), axis=0)
    grad_weight = local_grad / rows_dev
    return (grad_rows, grad_weight)


def solution(mesh):
    sizes = [size for _, size in DP_PARTS]
    devices = mesh.devices.reshape(*sizes, mesh.devices.shape[1])
    parted = Mesh(devices, (*DP, "bin"))
    return jax.shard_map(
        local,
        mesh=parted,
        in_specs=(P((*DP, "bin"), None, None), P("bin", None), P((*DP, "bin"), None), P(), P()),
        out_specs=(P((*DP, "bin"), None, None), P(("bin", *DP), None)),
        check_vma=False,
    )
```

```python
import jax
import jax.numpy as jnp
from jax import lax
from jax.sharding import Mesh
from jax.sharding import PartitionSpec as P

MOSTB = 2


SOFTMAX_TEMP_SCALE = 0.1

DP_PARTS = (("dx", 4), ("dz", 16), ("dc", 2))
DP = tuple(name for name, _ in DP_PARTS)
EMPTY_MARK = 4.0


def allowed_mask(valid, first, bin_link, group_slots, per_bin):
    per_owner = per_bin * MOSTB
    position = jnp.arange(group_slots, dtype=jnp.int32)
    local_bin = position % per_owner // per_bin
    padded = jnp.concatenate([bin_link, jnp.zeros((MOSTB,), jnp.int32)])
    nearby = lax.dynamic_slice(padded, (first,), (MOSTB,))
    lower = jnp.minimum(local_bin[:, None], local_bin[None, :])
    linked = jnp.zeros((group_slots, group_slots), jnp.int32)
    for height in range(MOSTB):
        linked = linked + jnp.where(lower == height, nearby[height], 0)
    spacing = jnp.abs(local_bin[:, None] - local_bin[None, :])
    paired = valid[:, None] & valid[None, :]
    allowed = paired & ((spacing == 0) | (spacing == 1) & (linked == 1))
    allowed = allowed | (position[:, None] == position[None, :])
    return allowed.astype(jnp.float32)


def contrast(query_rows, key_matrix, allowed, valid):
    similarity_scores = (
        lax.dot_general(
            query_rows, key_matrix, (((1,), (1,)), ((), ())), preferred_element_type=jnp.float32
        )
        / SOFTMAX_TEMP_SCALE
    )
    weights = allowed * jnp.exp(similarity_scores)
    shares = weights / jnp.sum(weights, axis=1, keepdims=True)
    position = jnp.arange(query_rows.shape[0], dtype=jnp.int32)
    diagonal = (position[:, None] == position[None, :]).astype(jnp.float32)
    logit_gradient = ((shares - diagonal) * valid[:, None]).astype(jnp.bfloat16)
    query_gradient = (
        jnp.dot(logit_gradient, key_matrix, preferred_element_type=jnp.float32) / SOFTMAX_TEMP_SCALE
    ).astype(jnp.bfloat16)
    key_gradient_rows = (
        lax.dot_general(
            logit_gradient, query_rows, (((0,), (0,)), ((), ())), preferred_element_type=jnp.float32
        )
        / SOFTMAX_TEMP_SCALE
    ).astype(jnp.bfloat16)
    return query_gradient, key_gradient_rows


def dp_index():
    index = 0
    for name, size in DP_PARTS:
        index = index * size + lax.axis_index(name)
    return index


def local(features, head_weight, bin_of_row, bin_owner, bin_link):
    rows_dev, views, feat_dim = features.shape
    part_rows, emb_dim = head_weight.shape
    sources = 1
    for _, size in DP_PARTS:
        sources *= size
    bins_n = lax.axis_size("bin")
    bin_count = bin_owner.shape[0]
    per_bin = max(2, 2 * rows_dev // bin_count)
    per_owner = per_bin * MOSTB
    group_slots = sources * per_owner
    flat = features.reshape(rows_dev * views, feat_dim)
    core = lax.axis_index("dc")
    halves = head_weight.reshape(2, part_rows // 2, emb_dim)
    half = lax.dynamic_index_in_dim(halves, core, 0, keepdims=False)
    copies = jnp.broadcast_to(half[None], (bins_n, part_rows // 2, emb_dim))
    mine = lax.all_to_all(copies, "bin", split_axis=0, concat_axis=0, tiled=True)
    theirs = lax.ppermute(mine, "dc", perm=[(0, 1), (1, 0)])
    quarters = flat.reshape(rows_dev * views, bins_n, 2, part_rows // 2)
    own_cols = lax.dynamic_index_in_dim(quarters, core, 2, keepdims=False)
    other_cols = lax.dynamic_index_in_dim(quarters, 1 - core, 2, keepdims=False)
    contract = (((1, 2), (0, 1)), ((), ()))
    folded = lax.dot_general(own_cols, mine, contract, preferred_element_type=jnp.float32)
    folded = folded + lax.dot_general(other_cols, theirs, contract, preferred_element_type=jnp.float32)
    embedded = folded.reshape(rows_dev, views, emb_dim)
    scale = lax.rsqrt(jnp.sum(embedded * embedded, axis=2, keepdims=True) + 1e-06)
    unit = embedded * scale
    sent = unit.astype(jnp.bfloat16)
    row_bins = bin_of_row[:, 0]
    lookup = row_bins[:, None] == jnp.arange(bin_count, dtype=jnp.int32)[None, :]
    owner = jnp.sum(jnp.where(lookup, bin_owner[None, :], 0), axis=1)
    first_by_bin = jnp.sum((bin_owner[None, :] < bin_owner[:, None]).astype(jnp.int32), axis=1)
    local_bin = row_bins - jnp.sum(jnp.where(lookup, first_by_bin[None, :], 0), axis=1)
    order = jnp.arange(rows_dev, dtype=jnp.int32)
    earlier = (row_bins[:, None] == row_bins[None, :]) & (order[None, :] < order[:, None])
    seat = jnp.sum(earlier.astype(jnp.int32), axis=1)
    target = owner * per_owner + local_bin * per_bin + seat
    block = views * per_owner
    dest = (
        (target // per_owner)[:, None] * block
        + jnp.arange(views, dtype=jnp.int32)[None, :] * per_owner
        + (target % per_owner)[:, None]
    )
    lanes = sources * block
    picks = (dest.reshape(-1)[None, :] == jnp.arange(lanes, dtype=jnp.int32)[:, None]).astype(jnp.bfloat16)
    picked = jnp.dot(
        picks, sent.reshape(rows_dev * views, emb_dim), preferred_element_type=jnp.float32
    )
    unfilled = 1.0 - jnp.sum(picks.astype(jnp.float32), axis=1)
    lane_view = jnp.arange(lanes, dtype=jnp.int32) % block // per_owner
    marked = unfilled * (lane_view == 0).astype(jnp.float32) * EMPTY_MARK
    first_lane = (jnp.arange(emb_dim, dtype=jnp.int32) == 0).astype(jnp.float32)
    outbox = (picked + marked[:, None] * first_lane[None, :]).astype(jnp.bfloat16)
    inbox = lax.all_to_all(
        outbox.reshape(sources, block, emb_dim), DP, split_axis=0, concat_axis=0, tiled=True
    )
    inbox = inbox.reshape(sources, views, per_owner, emb_dim)
    valid = (inbox[:, 0, :, 0] < 2.0).reshape(group_slots)
    query = inbox[:, 0].reshape(group_slots, emb_dim)
    key = inbox[:, 1].reshape(group_slots, emb_dim)
    first = jnp.sum((bin_owner < dp_index()).astype(jnp.int32))
    allowed = allowed_mask(valid, first, bin_link, group_slots, per_bin)
    grads = contrast(query, key, allowed, valid.astype(jnp.float32))
    back = jnp.stack([g.reshape(sources, per_owner, emb_dim) for g in grads], axis=1)
    returned = lax.all_to_all(
        back.reshape(sources, block, emb_dim), DP, split_axis=0, concat_axis=0, tiled=True
    )
    row_grads = lax.dot_general(
        picks,
        returned.reshape(lanes, emb_dim),
        (((0,), (0,)), ((), ())),
        preferred_element_type=jnp.float32,
    ).reshape(rows_dev, views, emb_dim)
    grad_rows = (
        scale * (row_grads - unit * jnp.sum(unit * row_grads, axis=2, keepdims=True))
    ).astype(jnp.bfloat16)
    column_start = lax.axis_index("bin") * part_rows
    trunk = lax.all_gather(features, "bin", axis=0, tiled=True)
    outgrad = lax.all_to_all(
        jnp.broadcast_to(grad_rows[None], (bins_n, *grad_rows.shape)),
        "bin",
        split_axis=0,
        concat_axis=0,
        tiled=True,
    )
    columns = lax.dynamic_slice_in_dim(trunk, column_start, part_rows, 2)
    count = trunk.shape[0]
    local_grad = lax.dot_general(
        columns.reshape(count * views, part_rows),
        outgrad.reshape(count * views, emb_dim),
        (((0,), (0,)), ((), ())),
        preferred_element_type=jnp.float32,
    )
    sizes = [size for _, size in DP_PARTS]
    per_dev = part_rows // sources
    local_grad = jnp.transpose(local_grad.reshape(*sizes, per_dev, emb_dim), (2, 0, 1, 3, 4))
    kept = lax.dynamic_index_in_dim(local_grad, core, 0, keepdims=False)
    given = lax.dynamic_index_in_dim(local_grad, 1 - core, 0, keepdims=False)
    local_grad = kept + lax.ppermute(given, "dc", perm=[(0, 1), (1, 0)])
    planes = local_grad.reshape(sizes[0], sizes[1] * per_dev, emb_dim).astype(jnp.bfloat16)
    planes = lax.all_to_all(planes, "dx", split_axis=0, concat_axis=0, tiled=True)
    planes = jnp.sum(planes.astype(jnp.float32), axis=0)
    planes = planes.reshape(sizes[1], per_dev, emb_dim).astype(jnp.bfloat16)
    planes = lax.all_to_all(planes, "dz", split_axis=0, concat_axis=0, tiled=True)
    local_grad = jnp.sum(planes.astype(jnp.float32), axis=0)
    grad_weight = local_grad / rows_dev
    return (grad_rows, grad_weight)


def solution(mesh):
    sizes = [size for _, size in DP_PARTS]
    devices = mesh.devices.reshape(*sizes, mesh.devices.shape[1])
    parted = Mesh(devices, (*DP, "bin"))
    return jax.shard_map(
        local,
        mesh=parted,
        in_specs=(P((*DP, "bin"), None, None), P("bin", None), P((*DP, "bin"), None), P(), P()),
        out_specs=(P((*DP, "bin"), None, None), P(("bin", *DP), None)),
        check_vma=False,
    )
```

```python
import jax
import jax.numpy as jnp
from jax import lax
from jax.sharding import Mesh
from jax.sharding import PartitionSpec as P

MOSTB = 2


SOFTMAX_TEMP_SCALE = 0.1

DP_PARTS = (("dx", 4), ("dz", 16), ("dc", 2))
DP = tuple(name for name, _ in DP_PARTS)
EMPTY_MARK = 4.0


def allowed_mask(valid, first, bin_link, group_slots, per_bin):
    per_owner = per_bin * MOSTB
    position = jnp.arange(group_slots, dtype=jnp.int32)
    local_bin = position % per_owner // per_bin
    padded = jnp.concatenate([bin_link, jnp.zeros((MOSTB,), jnp.int32)])
    nearby = lax.dynamic_slice(padded, (first,), (MOSTB,))
    lower = jnp.minimum(local_bin[:, None], local_bin[None, :])
    linked = jnp.zeros((group_slots, group_slots), jnp.int32)
    for height in range(MOSTB):
        linked = linked + jnp.where(lower == height, nearby[height], 0)
    spacing = jnp.abs(local_bin[:, None] - local_bin[None, :])
    paired = valid[:, None] & valid[None, :]
    allowed = paired & ((spacing == 0) | (spacing == 1) & (linked == 1))
    allowed = allowed | (position[:, None] == position[None, :])
    return allowed.astype(jnp.float32)


def contrast(query_rows, key_matrix, allowed, valid):
    similarity_scores = (
        lax.dot_general(
            query_rows, key_matrix, (((1,), (1,)), ((), ())), preferred_element_type=jnp.float32
        )
        / SOFTMAX_TEMP_SCALE
    )
    weights = allowed * jnp.exp(similarity_scores)
    shares = weights / jnp.sum(weights, axis=1, keepdims=True)
    position = jnp.arange(query_rows.shape[0], dtype=jnp.int32)
    diagonal = (position[:, None] == position[None, :]).astype(jnp.float32)
    logit_gradient = ((shares - diagonal) * valid[:, None]).astype(jnp.bfloat16)
    query_gradient = (
        jnp.dot(logit_gradient, key_matrix, preferred_element_type=jnp.float32) / SOFTMAX_TEMP_SCALE
    ).astype(jnp.bfloat16)
    key_gradient_rows = (
        lax.dot_general(
            logit_gradient, query_rows, (((0,), (0,)), ((), ())), preferred_element_type=jnp.float32
        )
        / SOFTMAX_TEMP_SCALE
    ).astype(jnp.bfloat16)
    return query_gradient, key_gradient_rows


def dp_index():
    index = 0
    for name, size in DP_PARTS:
        index = index * size + lax.axis_index(name)
    return index


def local(features, head_weight, bin_of_row, bin_owner, bin_link):
    rows_dev, views, feat_dim = features.shape
    part_rows, emb_dim = head_weight.shape
    sources = 1
    for _, size in DP_PARTS:
        sources *= size
    bins_n = lax.axis_size("bin")
    bin_count = bin_owner.shape[0]
    per_bin = max(2, 2 * rows_dev // bin_count)
    per_owner = per_bin * MOSTB
    group_slots = sources * per_owner
    flat = features.reshape(rows_dev * views, feat_dim)
    core = lax.axis_index("dc")
    halves = head_weight.reshape(2, part_rows // 2, emb_dim)
    half = lax.dynamic_index_in_dim(halves, core, 0, keepdims=False)
    copies = jnp.broadcast_to(half[None], (bins_n, part_rows // 2, emb_dim))
    mine = lax.all_to_all(copies, "bin", split_axis=0, concat_axis=0, tiled=True)
    theirs = lax.ppermute(mine, "dc", perm=[(0, 1), (1, 0)])
    low = jnp.where(core == 0, mine, theirs)
    high = jnp.where(core == 0, theirs, mine)
    weight = jnp.stack([low, high], axis=1).reshape(feat_dim, emb_dim)
    folded = jnp.dot(flat, weight, preferred_element_type=jnp.float32)
    embedded = folded.reshape(rows_dev, views, emb_dim)
    scale = lax.rsqrt(jnp.sum(embedded * embedded, axis=2, keepdims=True) + 1e-06)
    unit = embedded * scale
    sent = unit.astype(jnp.bfloat16)
    row_bins = bin_of_row[:, 0]
    lookup = row_bins[:, None] == jnp.arange(bin_count, dtype=jnp.int32)[None, :]
    owner = jnp.sum(jnp.where(lookup, bin_owner[None, :], 0), axis=1)
    first_by_bin = jnp.sum((bin_owner[None, :] < bin_owner[:, None]).astype(jnp.int32), axis=1)
    local_bin = row_bins - jnp.sum(jnp.where(lookup, first_by_bin[None, :], 0), axis=1)
    order = jnp.arange(rows_dev, dtype=jnp.int32)
    earlier = (row_bins[:, None] == row_bins[None, :]) & (order[None, :] < order[:, None])
    seat = jnp.sum(earlier.astype(jnp.int32), axis=1)
    target = owner * per_owner + local_bin * per_bin + seat
    block = views * per_owner
    dest = (
        (target // per_owner)[:, None] * block
        + jnp.arange(views, dtype=jnp.int32)[None, :] * per_owner
        + (target % per_owner)[:, None]
    )
    lanes = sources * block
    picks = (dest.reshape(-1)[None, :] == jnp.arange(lanes, dtype=jnp.int32)[:, None]).astype(jnp.bfloat16)
    picked = jnp.dot(
        picks, sent.reshape(rows_dev * views, emb_dim), preferred_element_type=jnp.float32
    )
    unfilled = 1.0 - jnp.sum(picks.astype(jnp.float32), axis=1)
    lane_view = jnp.arange(lanes, dtype=jnp.int32) % block // per_owner
    marked = unfilled * (lane_view == 0).astype(jnp.float32) * EMPTY_MARK
    first_lane = (jnp.arange(emb_dim, dtype=jnp.int32) == 0).astype(jnp.float32)
    outbox = (picked + marked[:, None] * first_lane[None, :]).astype(jnp.bfloat16)
    inbox = lax.all_to_all(
        outbox.reshape(sources, block, emb_dim), DP, split_axis=0, concat_axis=0, tiled=True
    )
    inbox = inbox.reshape(sources, views, per_owner, emb_dim)
    valid = (inbox[:, 0, :, 0] < 2.0).reshape(group_slots)
    query = inbox[:, 0].reshape(group_slots, emb_dim)
    key = inbox[:, 1].reshape(group_slots, emb_dim)
    first = jnp.sum((bin_owner < dp_index()).astype(jnp.int32))
    allowed = allowed_mask(valid, first, bin_link, group_slots, per_bin)
    grads = contrast(query, key, allowed, valid.astype(jnp.float32))
    back = jnp.stack([g.reshape(sources, per_owner, emb_dim) for g in grads], axis=1)
    own_bin = lax.axis_index("bin")
    chunks = flat.reshape(rows_dev * views, bins_n, part_rows)
    sends = [
        lax.dynamic_index_in_dim(chunks, (own_bin + shift) % bins_n, 1, keepdims=False)
        for shift in range(bins_n)
    ]
    back, sends = lax.optimization_barrier((back, sends))
    returned = lax.all_to_all(
        back.reshape(sources, block, emb_dim), DP, split_axis=0, concat_axis=0, tiled=True
    )
    arrived = [sends[0]] + [
        lax.ppermute(sends[shift], "bin", perm=[(j, (j + shift) % bins_n) for j in range(bins_n)])
        for shift in range(1, bins_n)
    ]
    returned, arrived = lax.optimization_barrier((returned, arrived))
    by_source = (own_bin - jnp.arange(bins_n, dtype=jnp.int32)) % bins_n
    columns = jnp.take(jnp.stack(arrived), by_source, axis=0).reshape(-1, part_rows)
    row_grads = lax.dot_general(
        picks,
        returned.reshape(lanes, emb_dim),
        (((0,), (0,)), ((), ())),
        preferred_element_type=jnp.float32,
    ).reshape(rows_dev, views, emb_dim)
    grad_rows = (
        scale * (row_grads - unit * jnp.sum(unit * row_grads, axis=2, keepdims=True))
    ).astype(jnp.bfloat16)
    outgrad = lax.all_to_all(
        jnp.broadcast_to(grad_rows[None], (bins_n, *grad_rows.shape)),
        "bin",
        split_axis=0,
        concat_axis=0,
        tiled=True,
    )
    local_grad = lax.dot_general(
        columns,
        outgrad.reshape(-1, emb_dim),
        (((0,), (0,)), ((), ())),
        preferred_element_type=jnp.float32,
    )
    sizes = [size for _, size in DP_PARTS]
    per_dev = part_rows // sources
    local_grad = jnp.transpose(local_grad.reshape(*sizes, per_dev, emb_dim), (2, 0, 1, 3, 4))
    kept = lax.dynamic_index_in_dim(local_grad, core, 0, keepdims=False)
    given = lax.dynamic_index_in_dim(local_grad, 1 - core, 0, keepdims=False)
    local_grad = kept + lax.ppermute(given, "dc", perm=[(0, 1), (1, 0)])
    planes = local_grad.reshape(sizes[0], sizes[1] * per_dev, emb_dim).astype(jnp.bfloat16)
    planes = lax.all_to_all(planes, "dx", split_axis=0, concat_axis=0, tiled=True)
    planes = jnp.sum(planes.astype(jnp.float32), axis=0)
    planes = planes.reshape(sizes[1], per_dev, emb_dim).astype(jnp.bfloat16)
    planes = lax.all_to_all(planes, "dz", split_axis=0, concat_axis=0, tiled=True)
    local_grad = jnp.sum(planes.astype(jnp.float32), axis=0)
    grad_weight = local_grad / rows_dev
    return (grad_rows, grad_weight)


def solution(mesh):
    sizes = [size for _, size in DP_PARTS]
    devices = mesh.devices.reshape(*sizes, mesh.devices.shape[1])
    parted = Mesh(devices, (*DP, "bin"))
    return jax.shard_map(
        local,
        mesh=parted,
        in_specs=(P((*DP, "bin"), None, None), P("bin", None), P((*DP, "bin"), None), P(), P()),
        out_specs=(P((*DP, "bin"), None, None), P(("bin", *DP), None)),
        check_vma=False,
    )
```

```python
import jax
import jax.numpy as jnp
from jax import lax
from jax.sharding import Mesh
from jax.sharding import PartitionSpec as P

MOSTB = 2


SOFTMAX_TEMP_SCALE = 0.1

DP_PARTS = (("dx", 4), ("dz", 16), ("dc", 2))
DP = tuple(name for name, _ in DP_PARTS)
EMPTY_MARK = 4.0


def allowed_mask(valid, first, bin_link, group_slots, per_bin):
    per_owner = per_bin * MOSTB
    position = jnp.arange(group_slots, dtype=jnp.int32)
    local_bin = position % per_owner // per_bin
    padded = jnp.concatenate([bin_link, jnp.zeros((MOSTB,), jnp.int32)])
    nearby = lax.dynamic_slice(padded, (first,), (MOSTB,))
    lower = jnp.minimum(local_bin[:, None], local_bin[None, :])
    linked = jnp.zeros((group_slots, group_slots), jnp.int32)
    for height in range(MOSTB):
        linked = linked + jnp.where(lower == height, nearby[height], 0)
    spacing = jnp.abs(local_bin[:, None] - local_bin[None, :])
    paired = valid[:, None] & valid[None, :]
    allowed = paired & ((spacing == 0) | (spacing == 1) & (linked == 1))
    allowed = allowed | (position[:, None] == position[None, :])
    return allowed.astype(jnp.float32)


def contrast(query_rows, key_matrix, allowed, valid):
    similarity_scores = (
        lax.dot_general(
            query_rows, key_matrix, (((1,), (1,)), ((), ())), preferred_element_type=jnp.float32
        )
        / SOFTMAX_TEMP_SCALE
    )
    weights = allowed * jnp.exp(similarity_scores)
    shares = weights / jnp.sum(weights, axis=1, keepdims=True)
    position = jnp.arange(query_rows.shape[0], dtype=jnp.int32)
    diagonal = (position[:, None] == position[None, :]).astype(jnp.float32)
    logit_gradient = ((shares - diagonal) * valid[:, None]).astype(jnp.bfloat16)
    query_gradient = (
        jnp.dot(logit_gradient, key_matrix, preferred_element_type=jnp.float32) / SOFTMAX_TEMP_SCALE
    ).astype(jnp.bfloat16)
    key_gradient_rows = (
        lax.dot_general(
            logit_gradient, query_rows, (((0,), (0,)), ((), ())), preferred_element_type=jnp.float32
        )
        / SOFTMAX_TEMP_SCALE
    ).astype(jnp.bfloat16)
    return query_gradient, key_gradient_rows


def dp_index():
    index = 0
    for name, size in DP_PARTS:
        index = index * size + lax.axis_index(name)
    return index


def local(features, head_weight, bin_of_row, bin_owner, bin_link):
    rows_dev, views, feat_dim = features.shape
    part_rows, emb_dim = head_weight.shape
    sources = 1
    for _, size in DP_PARTS:
        sources *= size
    bins_n = lax.axis_size("bin")
    bin_count = bin_owner.shape[0]
    per_bin = max(2, 2 * rows_dev // bin_count)
    per_owner = per_bin * MOSTB
    group_slots = sources * per_owner
    flat = features.reshape(rows_dev * views, feat_dim)
    core = lax.axis_index("dc")
    halves = head_weight.reshape(2, part_rows // 2, emb_dim)
    half = lax.dynamic_index_in_dim(halves, core, 0, keepdims=False)
    copies = jnp.broadcast_to(half[None], (bins_n, part_rows // 2, emb_dim))
    mine = lax.all_to_all(copies, "bin", split_axis=0, concat_axis=0, tiled=True)
    theirs = lax.ppermute(mine, "dc", perm=[(0, 1), (1, 0)])
    low = jnp.where(core == 0, mine, theirs)
    high = jnp.where(core == 0, theirs, mine)
    weight = jnp.stack([low, high], axis=1).reshape(feat_dim, emb_dim)
    folded = jnp.dot(flat, weight, preferred_element_type=jnp.float32)
    embedded = folded.reshape(rows_dev, views, emb_dim)
    scale = lax.rsqrt(jnp.sum(embedded * embedded, axis=2, keepdims=True) + 1e-06)
    unit = embedded * scale
    sent = unit.astype(jnp.bfloat16)
    row_bins = bin_of_row[:, 0]
    lookup = row_bins[:, None] == jnp.arange(bin_count, dtype=jnp.int32)[None, :]
    owner = jnp.sum(jnp.where(lookup, bin_owner[None, :], 0), axis=1)
    first_by_bin = jnp.sum((bin_owner[None, :] < bin_owner[:, None]).astype(jnp.int32), axis=1)
    local_bin = row_bins - jnp.sum(jnp.where(lookup, first_by_bin[None, :], 0), axis=1)
    order = jnp.arange(rows_dev, dtype=jnp.int32)
    earlier = (row_bins[:, None] == row_bins[None, :]) & (order[None, :] < order[:, None])
    seat = jnp.sum(earlier.astype(jnp.int32), axis=1)
    target = owner * per_owner + local_bin * per_bin + seat
    block = views * per_owner
    dest = (
        (target // per_owner)[:, None] * block
        + jnp.arange(views, dtype=jnp.int32)[None, :] * per_owner
        + (target % per_owner)[:, None]
    )
    lanes = sources * block
    picks = (dest.reshape(-1)[None, :] == jnp.arange(lanes, dtype=jnp.int32)[:, None]).astype(jnp.bfloat16)
    picked = jnp.dot(
        picks, sent.reshape(rows_dev * views, emb_dim), preferred_element_type=jnp.float32
    )
    unfilled = 1.0 - jnp.sum(picks.astype(jnp.float32), axis=1)
    lane_view = jnp.arange(lanes, dtype=jnp.int32) % block // per_owner
    marked = unfilled * (lane_view == 0).astype(jnp.float32) * EMPTY_MARK
    first_lane = (jnp.arange(emb_dim, dtype=jnp.int32) == 0).astype(jnp.float32)
    outbox = (picked + marked[:, None] * first_lane[None, :]).astype(jnp.bfloat16)
    inbox = lax.all_to_all(
        outbox.reshape(sources, block, emb_dim), DP, split_axis=0, concat_axis=0, tiled=True
    )
    inbox = inbox.reshape(sources, views, per_owner, emb_dim)
    valid = (inbox[:, 0, :, 0] < 2.0).reshape(group_slots)
    query = inbox[:, 0].reshape(group_slots, emb_dim)
    key = inbox[:, 1].reshape(group_slots, emb_dim)
    first = jnp.sum((bin_owner < dp_index()).astype(jnp.int32))
    allowed = allowed_mask(valid, first, bin_link, group_slots, per_bin)
    grads = contrast(query, key, allowed, valid.astype(jnp.float32))
    back = jnp.stack([g.reshape(sources, per_owner, emb_dim) for g in grads], axis=1)
    own_bin = lax.axis_index("bin")
    chunks = flat.reshape(rows_dev * views, bins_n, part_rows)
    sends = [
        lax.dynamic_index_in_dim(chunks, (own_bin + shift) % bins_n, 1, keepdims=False)
        for shift in range(bins_n)
    ]
    back, sends = lax.optimization_barrier((back, sends))
    returned = lax.all_to_all(
        back.reshape(sources, block, emb_dim), DP, split_axis=0, concat_axis=0, tiled=True
    )
    arrived = [sends[0]] + [
        lax.ppermute(sends[shift], "bin", perm=[(j, (j + shift) % bins_n) for j in range(bins_n)])
        for shift in range(1, bins_n)
    ]
    returned, arrived = lax.optimization_barrier((returned, arrived))
    by_source = (own_bin - jnp.arange(bins_n, dtype=jnp.int32)) % bins_n
    columns = jnp.take(jnp.stack(arrived), by_source, axis=0).reshape(-1, part_rows)
    row_grads = lax.dot_general(
        picks,
        returned.reshape(lanes, emb_dim),
        (((0,), (0,)), ((), ())),
        preferred_element_type=jnp.float32,
    ).reshape(rows_dev, views, emb_dim)
    grad_rows = (
        scale * (row_grads - unit * jnp.sum(unit * row_grads, axis=2, keepdims=True))
    ).astype(jnp.bfloat16)
    given_rows = [grad_rows] + [
        lax.ppermute(grad_rows, "bin", perm=[(j, (j + shift) % bins_n) for j in range(bins_n)])
        for shift in range(1, bins_n)
    ]
    outgrad = jnp.take(jnp.stack(given_rows), by_source, axis=0)
    local_grad = lax.dot_general(
        columns,
        outgrad.reshape(-1, emb_dim),
        (((0,), (0,)), ((), ())),
        preferred_element_type=jnp.float32,
    )
    sizes = [size for _, size in DP_PARTS]
    per_dev = part_rows // sources
    local_grad = jnp.transpose(local_grad.reshape(*sizes, per_dev, emb_dim), (2, 0, 1, 3, 4))
    kept = lax.dynamic_index_in_dim(local_grad, core, 0, keepdims=False)
    given = lax.dynamic_index_in_dim(local_grad, 1 - core, 0, keepdims=False)
    local_grad = kept + lax.ppermute(given, "dc", perm=[(0, 1), (1, 0)])
    planes = local_grad.reshape(sizes[0], sizes[1] * per_dev, emb_dim).astype(jnp.bfloat16)
    planes = lax.all_to_all(planes, "dx", split_axis=0, concat_axis=0, tiled=True)
    planes = jnp.sum(planes.astype(jnp.float32), axis=0)
    planes = planes.reshape(sizes[1], per_dev, emb_dim).astype(jnp.bfloat16)
    planes = lax.all_to_all(planes, "dz", split_axis=0, concat_axis=0, tiled=True)
    local_grad = jnp.sum(planes.astype(jnp.float32), axis=0)
    grad_weight = local_grad / rows_dev
    return (grad_rows, grad_weight)


def solution(mesh):
    sizes = [size for _, size in DP_PARTS]
    devices = mesh.devices.reshape(*sizes, mesh.devices.shape[1])
    parted = Mesh(devices, (*DP, "bin"))
    return jax.shard_map(
        local,
        mesh=parted,
        in_specs=(P((*DP, "bin"), None, None), P("bin", None), P((*DP, "bin"), None), P(), P()),
        out_specs=(P((*DP, "bin"), None, None), P(("bin", *DP), None)),
        check_vma=False,
    )
```

```python
import jax
import jax.numpy as jnp
from jax import lax
from jax.sharding import Mesh
from jax.sharding import PartitionSpec as P

MOSTB = 2


SOFTMAX_TEMP_SCALE = 0.1

DP_PARTS = (("dx", 4), ("dz", 16), ("dc", 2))
DP = tuple(name for name, _ in DP_PARTS)
EMPTY_MARK = 4.0


def allowed_mask(valid, first, bin_link, group_slots, per_bin):
    per_owner = per_bin * MOSTB
    position = jnp.arange(group_slots, dtype=jnp.int32)
    local_bin = position % per_owner // per_bin
    padded = jnp.concatenate([bin_link, jnp.zeros((MOSTB,), jnp.int32)])
    nearby = lax.dynamic_slice(padded, (first,), (MOSTB,))
    lower = jnp.minimum(local_bin[:, None], local_bin[None, :])
    linked = jnp.zeros((group_slots, group_slots), jnp.int32)
    for height in range(MOSTB):
        linked = linked + jnp.where(lower == height, nearby[height], 0)
    spacing = jnp.abs(local_bin[:, None] - local_bin[None, :])
    paired = valid[:, None] & valid[None, :]
    allowed = paired & ((spacing == 0) | (spacing == 1) & (linked == 1))
    allowed = allowed | (position[:, None] == position[None, :])
    return allowed.astype(jnp.float32)


def contrast(query_rows, key_matrix, allowed, valid):
    similarity_scores = (
        lax.dot_general(
            query_rows, key_matrix, (((1,), (1,)), ((), ())), preferred_element_type=jnp.float32
        )
        / SOFTMAX_TEMP_SCALE
    )
    weights = allowed * jnp.exp(similarity_scores)
    shares = weights / jnp.sum(weights, axis=1, keepdims=True)
    position = jnp.arange(query_rows.shape[0], dtype=jnp.int32)
    diagonal = (position[:, None] == position[None, :]).astype(jnp.float32)
    logit_gradient = ((shares - diagonal) * valid[:, None]).astype(jnp.bfloat16)
    query_gradient = (
        jnp.dot(logit_gradient, key_matrix, preferred_element_type=jnp.float32) / SOFTMAX_TEMP_SCALE
    ).astype(jnp.bfloat16)
    key_gradient_rows = (
        lax.dot_general(
            logit_gradient, query_rows, (((0,), (0,)), ((), ())), preferred_element_type=jnp.float32
        )
        / SOFTMAX_TEMP_SCALE
    ).astype(jnp.bfloat16)
    return query_gradient, key_gradient_rows


def dp_index():
    index = 0
    for name, size in DP_PARTS:
        index = index * size + lax.axis_index(name)
    return index


def local(features, head_weight, bin_of_row, bin_owner, bin_link):
    rows_dev, views, feat_dim = features.shape
    part_rows, emb_dim = head_weight.shape
    sources = 1
    for _, size in DP_PARTS:
        sources *= size
    bins_n = lax.axis_size("bin")
    bin_count = bin_owner.shape[0]
    per_bin = max(2, 2 * rows_dev // bin_count)
    per_owner = per_bin * MOSTB
    group_slots = sources * per_owner
    flat = features.reshape(rows_dev * views, feat_dim)
    core = lax.axis_index("dc")
    halves = head_weight.reshape(2, part_rows // 2, emb_dim)
    half = lax.dynamic_index_in_dim(halves, core, 0, keepdims=False)
    copies = jnp.broadcast_to(half[None], (bins_n, part_rows // 2, emb_dim))
    mine = lax.all_to_all(copies, "bin", split_axis=0, concat_axis=0, tiled=True)
    theirs = lax.ppermute(mine, "dc", perm=[(0, 1), (1, 0)])
    low = jnp.where(core == 0, mine, theirs)
    high = jnp.where(core == 0, theirs, mine)
    weight = jnp.stack([low, high], axis=1).reshape(feat_dim, emb_dim)
    folded = jnp.dot(flat, weight, preferred_element_type=jnp.float32)
    embedded = folded.reshape(rows_dev, views, emb_dim)
    scale = lax.rsqrt(jnp.sum(embedded * embedded, axis=2, keepdims=True) + 1e-06)
    unit = embedded * scale
    sent = unit.astype(jnp.bfloat16)
    row_bins = bin_of_row[:, 0]
    lookup = row_bins[:, None] == jnp.arange(bin_count, dtype=jnp.int32)[None, :]
    owner = jnp.sum(jnp.where(lookup, bin_owner[None, :], 0), axis=1)
    first_by_bin = jnp.sum((bin_owner[None, :] < bin_owner[:, None]).astype(jnp.int32), axis=1)
    local_bin = row_bins - jnp.sum(jnp.where(lookup, first_by_bin[None, :], 0), axis=1)
    order = jnp.arange(rows_dev, dtype=jnp.int32)
    earlier = (row_bins[:, None] == row_bins[None, :]) & (order[None, :] < order[:, None])
    seat = jnp.sum(earlier.astype(jnp.int32), axis=1)
    target = owner * per_owner + local_bin * per_bin + seat
    block = views * per_owner
    dest = (
        (target // per_owner)[:, None] * block
        + jnp.arange(views, dtype=jnp.int32)[None, :] * per_owner
        + (target % per_owner)[:, None]
    )
    lanes = sources * block
    picks = (dest.reshape(-1)[None, :] == jnp.arange(lanes, dtype=jnp.int32)[:, None]).astype(jnp.bfloat16)
    picked = jnp.dot(
        picks, sent.reshape(rows_dev * views, emb_dim), preferred_element_type=jnp.float32
    )
    unfilled = 1.0 - jnp.sum(picks.astype(jnp.float32), axis=1)
    lane_view = jnp.arange(lanes, dtype=jnp.int32) % block // per_owner
    marked = unfilled * (lane_view == 0).astype(jnp.float32) * EMPTY_MARK
    first_lane = (jnp.arange(emb_dim, dtype=jnp.int32) == 0).astype(jnp.float32)
    outbox = (picked + marked[:, None] * first_lane[None, :]).astype(jnp.bfloat16)
    inbox = lax.all_to_all(
        outbox.reshape(sources, block, emb_dim), DP, split_axis=0, concat_axis=0, tiled=True
    )
    inbox = inbox.reshape(sources, views, per_owner, emb_dim)
    valid = (inbox[:, 0, :, 0] < 2.0).reshape(group_slots)
    query = inbox[:, 0].reshape(group_slots, emb_dim)
    key = inbox[:, 1].reshape(group_slots, emb_dim)
    first = jnp.sum((bin_owner < dp_index()).astype(jnp.int32))
    allowed = allowed_mask(valid, first, bin_link, group_slots, per_bin)
    grads = contrast(query, key, allowed, valid.astype(jnp.float32))
    back = jnp.stack([g.reshape(sources, per_owner, emb_dim) for g in grads], axis=1)
    own_bin = lax.axis_index("bin")
    chunks = flat.reshape(rows_dev * views, bins_n, part_rows)
    sends = [
        lax.dynamic_index_in_dim(chunks, (own_bin + shift) % bins_n, 1, keepdims=False)
        for shift in range(bins_n)
    ]
    back, sends = lax.optimization_barrier((back, sends))
    returned = lax.all_to_all(
        back.reshape(sources, block, emb_dim), DP, split_axis=0, concat_axis=0, tiled=True
    )
    arrived = [sends[0]] + [
        lax.ppermute(sends[shift], "bin", perm=[(j, (j + shift) % bins_n) for j in range(bins_n)])
        for shift in range(1, bins_n)
    ]
    returned, arrived = lax.optimization_barrier((returned, arrived))
    by_source = (own_bin - jnp.arange(bins_n, dtype=jnp.int32)) % bins_n
    columns = jnp.take(jnp.stack(arrived), by_source, axis=0).reshape(-1, part_rows)
    row_grads = lax.dot_general(
        picks,
        returned.reshape(lanes, emb_dim),
        (((0,), (0,)), ((), ())),
        preferred_element_type=jnp.float32,
    ).reshape(rows_dev, views, emb_dim)
    grad_rows = (
        scale * (row_grads - unit * jnp.sum(unit * row_grads, axis=2, keepdims=True))
    ).astype(jnp.bfloat16)
    outgrad = lax.all_to_all(
        jnp.broadcast_to(grad_rows[None], (bins_n, *grad_rows.shape)),
        "bin",
        split_axis=0,
        concat_axis=0,
        tiled=True,
    )
    local_grad = lax.dot_general(
        columns,
        outgrad.reshape(-1, emb_dim),
        (((0,), (0,)), ((), ())),
        preferred_element_type=jnp.float32,
    )
    sizes = [size for _, size in DP_PARTS]
    per_dev = part_rows // sources
    local_grad = jnp.transpose(local_grad.reshape(*sizes, per_dev, emb_dim), (2, 0, 1, 3, 4))
    kept = lax.dynamic_index_in_dim(local_grad, core, 0, keepdims=False)
    given = lax.dynamic_index_in_dim(local_grad, 1 - core, 0, keepdims=False)
    swapped = lax.ppermute(given.astype(jnp.bfloat16), "dc", perm=[(0, 1), (1, 0)])
    local_grad = kept + swapped.astype(jnp.float32)
    planes = local_grad.reshape(sizes[0], sizes[1] * per_dev, emb_dim).astype(jnp.bfloat16)
    planes = lax.all_to_all(planes, "dx", split_axis=0, concat_axis=0, tiled=True)
    planes = jnp.sum(planes.astype(jnp.float32), axis=0)
    planes = planes.reshape(sizes[1], per_dev, emb_dim).astype(jnp.bfloat16)
    planes = lax.all_to_all(planes, "dz", split_axis=0, concat_axis=0, tiled=True)
    local_grad = jnp.sum(planes.astype(jnp.float32), axis=0)
    grad_weight = local_grad / rows_dev
    return (grad_rows, grad_weight)


def solution(mesh):
    sizes = [size for _, size in DP_PARTS]
    devices = mesh.devices.reshape(*sizes, mesh.devices.shape[1])
    parted = Mesh(devices, (*DP, "bin"))
    return jax.shard_map(
        local,
        mesh=parted,
        in_specs=(P((*DP, "bin"), None, None), P("bin", None), P((*DP, "bin"), None), P(), P()),
        out_specs=(P((*DP, "bin"), None, None), P(("bin", *DP), None)),
        check_vma=False,
    )
```
